256 devices in a mesh: users: 32 (over y, z), heads: 8 (over x, core).
Axes of the slice: x: 4, y: 4, z: 8, core: 2. Of those that a mesh axis runs over, the one named last changes fastest.
Arguments:
- tokens: bfloat16 [32768, 1024], P('users', 'heads'), may hold values from -6 to 6
- cotangent: bfloat16 [32768, 1024], P('users', 'heads'), may hold values from -6 to 6
- gain: float32 [1024], replicated, may hold values from 0.1 to 1.9
- w_proj: bfloat16 [1024, 16, 256], P(None, 'heads'), may hold values from -0.1875 to 0.1875
- w_out: bfloat16 [1024, 1024], P('heads'), may hold values from -0.1875 to 0.1875
- arrival_slot: int32 [256], replicated, may hold values from 0 to 255, as said below
- user_start: int32 [256], P('users'), may hold values from 0 to 7, as said below
- user_length: int32 [256], P('users'), may hold values from 1 to 1024, as said below
Outputs:
- mixed: bfloat16 [32768, 1024], P('users', 'heads')
- input_grad: bfloat16 [32768, 1024], P('users', 'heads')
- proj_grad: float32 [1024, 16, 256], P('users', 'heads')
- out_grad_t: float32 [1024, 1024], P('users', 'heads')
The draws below stay inside these ranges and needn't reach their ends.
Inputs may be any that keep to these rules, and one draw needn't show every extreme that they name: A permutation: arriving tile t goes to owner arrival_slot[t] // 8 as its tile arrival_slot[t] % 8. From one users-device to one owner go either no tiles or exactly 1. The tiles of one user are consecutive tiles of one owner; user_start is the same on all of them and equals the offset of the first. `user_length`: the same on all tiles of one user; a user of n tiles has more than (n - 1) * 128 events; some user has 1024 events.
All inputs are finite; a program needn't handle non-finite values.
Results may differ from the reference program's by a relative error of at most 0.011.
Values may be sent and summed in bfloat16 or wider, within the bound.
No kernel may reach another device: no remote copies, remote signals or barrier semaphores. Data moves between devices by JAX's collectives and lax.ppermute only.
A program may use at most 128 MiB of HBM per device.

```python
import math
import jax
import jax.numpy as jnp
from jax import lax

D = 1024
HEADS = 16
DH = 64
TILE = 128
CAP = 1
TD = 8
TILES = 256
ROWS = 32768


def owner_layout(key):
    groups = TILES // TD
    layout_key = jax.random.fold_in(key, 7)
    cut_key, trim_key, chosen_key = jax.random.split(layout_key, 3)
    place_ids = jnp.broadcast_to(jnp.arange(TD, dtype=jnp.int32)[None, :], (groups, TD))
    owner_ids = jnp.arange(groups, dtype=jnp.int32)[:, None]
    chosen = jax.random.randint(chosen_key, (), 0, groups)
    cut_marks = jax.random.randint(cut_key, (groups, TD), 0, 3) == 0
    starts = (place_ids == 0) | cut_marks & (owner_ids != chosen)
    first_tile = lax.cummax(jnp.where(starts, place_ids, 0), axis=1)
    same_user = first_tile[:, :, None] == first_tile[:, None, :]
    tiles_used = jnp.sum(same_user.astype(jnp.int32), axis=2)
    trim_draw = jax.random.randint(trim_key, (groups, TD), 0, TILE)
    trim_user = jnp.take_along_axis(trim_draw, first_tile, axis=1)
    trim_user = jnp.where(owner_ids == chosen, 0, trim_user)
    length = tiles_used * TILE - trim_user
    return (first_tile.reshape(-1).astype(jnp.int32), length.reshape(-1).astype(jnp.int32))


def draw_user_start(key, part):
    return owner_layout(key)[0]


def draw_user_length(key, part):
    return owner_layout(key)[1]


def draw_arrival_slot(key, part):
    groups = TILES // TD
    pair_count = TD // CAP
    slot_key = jax.random.fold_in(key, 11)
    source_key, order_key = jax.random.split(slot_key)
    compact_ids = jnp.arange(TILES, dtype=jnp.int32)
    owner_of = compact_ids // TD
    pair_of = compact_ids % TD // CAP
    within_pair = compact_ids % CAP
    pair_line = owner_of * pair_count + pair_of
    source_base = pair_line % groups
    slot_base = pair_line // groups * CAP + within_pair
    source_order = jax.random.permutation(source_key, groups).astype(jnp.int32)
    slot_order = jax.vmap(lambda sub_key: jax.random.permutation(sub_key, TD))(jax.random.split(order_key, groups)).astype(jnp.int32)
    source = source_order[source_base]
    arrival_ids = source * TD + slot_order[source, slot_base]
    return jnp.zeros((TILES,), jnp.int32).at[arrival_ids].set(compact_ids)


def block_levels(own_key, dims, pieces, low, largest):
    def one(dim, parts):
        draws = jax.random.uniform(jax.random.fold_in(jax.random.fold_in(own_key, 6), dim), (parts,), jnp.float32, low / len(pieces), largest / len(pieces))
        return jnp.repeat(jnp.exp(draws), dims[dim] // parts).reshape((-1,) + (1,) * (len(dims) - dim - 1))

    level = one(*pieces[0])
    for cut in pieces[1:]:
        level = level * one(*cut)
    return level


def noise(stream_key, extent, width, limit, cuts=(), held_as=jnp.bfloat16):
    result = width * jax.random.normal(stream_key, extent, jnp.float32)
    if cuts:
        result = result * block_levels(stream_key, extent, cuts, -0.22, 0.18)
    return jnp.clip(result, -limit, limit).astype(held_as)


def setup_inputs(seed: int = 0) -> dict:
    keys = jax.random.split(jax.random.key(seed), 9)
    tokens = noise(keys[0], (ROWS, D), 1.0, 6.0, ((0, 32), (1, 8)))
    cotangent = noise(keys[1], (ROWS, D), 1.0, 6.0, ((0, 32), (1, 8)))
    gain = jnp.clip(1.0 + 0.18 * jax.random.normal(keys[2], (D,), jnp.float32), 0.1, 1.9)
    w_proj = noise(keys[3], (D, HEADS, 4 * DH), D ** -0.5, 0.1875, ((1, 8),))
    w_out = noise(keys[4], (HEADS * DH, D), (HEADS * DH) ** -0.5, 0.1875, ((0, 8),))
    arrival_slot = draw_arrival_slot(jax.random.fold_in(keys[8], 71), 0)
    user_start = draw_user_start(jax.random.fold_in(keys[8], 71), 0)
    user_length = draw_user_length(jax.random.fold_in(keys[8], 71), 0)
    return {"tokens": tokens, "cotangent": cotangent, "gain": gain, "w_proj": w_proj, "w_out": w_out, "arrival_slot": arrival_slot, "user_start": user_start, "user_length": user_length}


norm_eps = 1e-05

def silu_slope(value):
    sigma = jax.nn.sigmoid(value)
    return sigma * (1.0 + value * (1.0 - sigma))

def owner_pass(own_tokens, own_cotangent, starts, lengths, gain, w_proj, w_out):
    rows = TD * TILE
    scale = DH ** (-0.5)
    tokens_wide = own_tokens.astype(jnp.float32)
    inv_rms = lax.rsqrt(lax.optimization_barrier(jnp.mean(tokens_wide * tokens_wide, axis=1, keepdims=True)) + norm_eps)
    normed = (tokens_wide * inv_rms * gain[None, :]).astype(jnp.bfloat16)
    proj_matrix = w_proj.reshape(D, HEADS * 4 * DH)
    projected = jnp.dot(normed, proj_matrix, preferred_element_type=jnp.float32).reshape(rows, HEADS, 4, DH)
    by_head = jnp.transpose(projected, (1, 2, 0, 3))
    gate_rows = jax.nn.silu(by_head[:, 0]).astype(jnp.bfloat16)
    value_rows = by_head[:, 1].astype(jnp.bfloat16)
    query_rows = jax.nn.silu(by_head[:, 2]).astype(jnp.bfloat16)
    key_rows = jax.nn.silu(by_head[:, 3]).astype(jnp.bfloat16)
    grad_mix = jnp.dot(own_cotangent, w_out.T, preferred_element_type=jnp.float32).astype(jnp.bfloat16)
    grad_mix = jnp.transpose(grad_mix.reshape(rows, HEADS, DH), (1, 0, 2))
    row_ids = jnp.arange(rows, dtype=jnp.int32)
    first = jnp.repeat(starts, TILE)
    length = jnp.repeat(lengths, TILE)
    position = (row_ids // TILE - first) * TILE + row_ids % TILE
    is_live = position < length
    allowed = (first[:, None] == first[None, :]) & (position[None, :] <= position[:, None]) & is_live[:, None] & is_live[None, :]
    length_wide = length.astype(jnp.float32)[:, None]

    def head_pass(operands):
        query_h, key_h, value_h, gate_h, grad_mix_h = operands
        scores = jnp.dot(query_h, key_h.T, preferred_element_type=jnp.float32) * scale
        weights = jnp.where(allowed, jax.nn.silu(scores) / length_wide, 0.0).astype(jnp.bfloat16)
        attended = jnp.dot(weights, value_h, preferred_element_type=jnp.float32)
        inv_attn = lax.rsqrt(lax.optimization_barrier(jnp.mean(attended * attended, axis=1, keepdims=True)) + norm_eps)
        attn_normed = attended * inv_attn
        gate_wide = gate_h.astype(jnp.float32)
        grad_mix_wide = grad_mix_h.astype(jnp.float32)
        mixer_h = (attn_normed * gate_wide).astype(jnp.bfloat16)
        grad_gate = grad_mix_wide * attn_normed
        grad_attn_normed = grad_mix_wide * gate_wide
        grad_attended = (inv_attn * (grad_attn_normed - attn_normed * lax.optimization_barrier(jnp.mean(grad_attn_normed * attn_normed, axis=1, keepdims=True)))).astype(jnp.bfloat16)
        grad_weights = jnp.dot(grad_attended, value_h.T, preferred_element_type=jnp.float32)
        grad_value = jnp.dot(weights.T, grad_attended, preferred_element_type=jnp.float32)
        grad_scores = jnp.where(allowed, grad_weights / length_wide * silu_slope(scores), 0.0).astype(jnp.bfloat16)
        grad_query = jnp.dot(grad_scores, key_h, preferred_element_type=jnp.float32) * scale
        grad_key = jnp.dot(grad_scores.T, query_h, preferred_element_type=jnp.float32) * scale
        return (mixer_h, grad_gate, grad_value, grad_query, grad_key)
    mixer_h, grad_gate, grad_value, grad_query, grad_key = lax.map(head_pass, (query_rows, key_rows, value_rows, gate_rows, grad_mix))
    grad_proj = jnp.stack([grad_gate * silu_slope(by_head[:, 0]), grad_value, grad_query * silu_slope(by_head[:, 2]), grad_key * silu_slope(by_head[:, 3])], axis=1)
    grad_proj = jnp.transpose(grad_proj, (2, 0, 1, 3)).astype(jnp.bfloat16).reshape(rows, HEADS * 4 * DH)
    mixer = jnp.transpose(mixer_h, (1, 0, 2)).reshape(rows, HEADS * DH)
    mixed = (tokens_wide + jnp.dot(mixer, w_out, preferred_element_type=jnp.float32)).astype(jnp.bfloat16)
    out_term = jnp.dot(own_cotangent.T, mixer, preferred_element_type=jnp.float32)
    proj_term = jnp.dot(normed.T, grad_proj, preferred_element_type=jnp.float32)
    grad_normed = jnp.dot(grad_proj, proj_matrix.T, preferred_element_type=jnp.float32)
    grad_scaled = grad_normed * gain[None, :]
    input_grad = (own_cotangent.astype(jnp.float32) + inv_rms * grad_scaled - tokens_wide * (inv_rms * inv_rms * inv_rms) * lax.optimization_barrier(jnp.mean(grad_scaled * tokens_wide, axis=1, keepdims=True))).astype(jnp.bfloat16)
    return (mixed, input_grad, proj_term, out_term)

def reference(tokens, cotangent, gain, w_proj, w_out, arrival_slot, user_start, user_length):
    groups = TILES // TD
    rows = TD * TILE
    inverse = jnp.zeros((TILES,), jnp.int32).at[arrival_slot].set(jnp.arange(TILES, dtype=jnp.int32))
    own_tokens = tokens.reshape(TILES, TILE, D)[inverse].reshape(groups, rows, D)
    own_cotangent = cotangent.reshape(TILES, TILE, D)[inverse].reshape(groups, rows, D)
    starts = user_start.reshape(groups, TD)
    lengths = user_length.reshape(groups, TD)

    def owner_step(carry, operands):
        proj_sum, out_sum = carry
        mixed, input_grad, proj_term, out_term = owner_pass(operands[0], operands[1], operands[2], operands[3], gain, w_proj, w_out)
        return ((proj_sum + proj_term, out_sum + out_term), (mixed, input_grad))
    start_sums = (jnp.zeros((D, HEADS * 4 * DH), jnp.float32), jnp.zeros((D, HEADS * DH), jnp.float32))
    (proj_sum, out_sum), (mixed, input_grad) = lax.scan(owner_step, start_sums, (own_tokens, own_cotangent, starts, lengths))
    norm_factor = 1.0 / math.sqrt(ROWS)
    mixed = mixed.reshape(TILES, TILE, D)[arrival_slot].reshape(ROWS, D)
    input_grad = input_grad.reshape(TILES, TILE, D)[arrival_slot].reshape(ROWS, D)
    return (mixed, input_grad, (proj_sum * norm_factor).reshape(D, HEADS, 4 * DH), out_sum * norm_factor)
```

```python
import math

import jax
import jax.numpy as jnp
from jax import lax
from jax.sharding import PartitionSpec as P

D = 1024
DH = 64
TILE = 128
CAP = 1


norm_eps = 1e-05


def silu_slope(value):
    sigma = jax.nn.sigmoid(value)
    return sigma * (1.0 + value * (1.0 - sigma))


def route_tables(arrival_slot, owner_index, groups, per_owner):
    placed = arrival_slot.reshape(groups, per_owner)
    owners = placed // per_owner
    tile_ids = jnp.arange(per_owner, dtype=jnp.int32)
    same_owner = owners[:, :, None] == owners[:, None, :]
    earlier = tile_ids[None, :] < tile_ids[:, None]
    ranks = jnp.sum((same_owner & earlier[None, :, :]).astype(jnp.int32), axis=2)
    my_owners = lax.dynamic_index_in_dim(owners, owner_index, 0, keepdims=False)
    my_ranks = lax.dynamic_index_in_dim(ranks, owner_index, 0, keepdims=False)
    buffer_ids = jnp.arange(groups * CAP, dtype=jnp.int32)
    peers = buffer_ids // CAP
    turns = buffer_ids % CAP
    chosen = (my_owners[None, :] == peers[:, None]) & (my_ranks[None, :] == turns[:, None])
    send_index = jnp.sum(chosen.astype(jnp.int32) * tile_ids[None, :], axis=1)
    send_valid = jnp.any(chosen, axis=1)
    codes = (jnp.arange(groups, dtype=jnp.int32)[:, None] * CAP + ranks).reshape(-1)
    wanted = owner_index * per_owner + tile_ids
    matches = placed.reshape(-1)[None, :] == wanted[:, None]
    receive_index = jnp.sum(matches.astype(jnp.int32) * codes[None, :], axis=1)
    owner_lines = jnp.repeat(owners, CAP, axis=0)
    rank_lines = jnp.repeat(ranks, CAP, axis=0)
    place_lines = jnp.repeat(placed, CAP, axis=0)
    returning = (owner_lines == owner_index) & (rank_lines == turns[:, None])
    back_index = jnp.sum(
        returning.astype(jnp.int32) * (place_lines - owner_index * per_owner), axis=1
    )
    back_valid = jnp.any(returning, axis=1)
    home_index = my_owners * CAP + my_ranks
    return (send_index, send_valid, receive_index, back_index, back_valid, home_index)


def select_tiles(tiles, index, keep):
    taken = jnp.take(tiles, index, axis=0)
    return jnp.where(keep[:, None, None], taken, jnp.zeros_like(taken))


def per_device(tokens, cotangent, gain, w_proj, w_out, arrival_slot, user_start, user_length):
    groups = lax.axis_size("users")
    owner_index = lax.axis_index("users")
    rows, width = tokens.shape
    per_owner = rows // TILE
    heads_here = w_proj.shape[1]
    scale = DH ** (-0.5)
    send_index, send_valid, receive_index, back_index, back_valid, home_index = route_tables(
        arrival_slot, owner_index, groups, per_owner
    )
    outgoing_tokens = select_tiles(tokens.reshape(per_owner, TILE, width), send_index, send_valid)
    outgoing_grads = select_tiles(cotangent.reshape(per_owner, TILE, width), send_index, send_valid)
    arrived = lax.all_to_all(
        jnp.stack([outgoing_tokens, outgoing_grads], axis=1),
        "users",
        split_axis=0,
        concat_axis=0,
        tiled=True,
    )
    own_tokens = jnp.take(arrived[:, 0], receive_index, axis=0).reshape(rows, width)
    own_cotangent = jnp.take(arrived[:, 1], receive_index, axis=0).reshape(rows, width)
    full_tokens, full_cotangent = (
        lax.all_gather(own_tokens, "heads", axis=1, tiled=True),
        lax.all_gather(own_cotangent, "heads", axis=1, tiled=True),
    )
    tokens_wide = full_tokens.astype(jnp.float32)
    inv_rms = lax.rsqrt(jnp.mean(tokens_wide * tokens_wide, axis=1, keepdims=True) + norm_eps)
    normed = (tokens_wide * inv_rms * gain[None, :]).astype(jnp.bfloat16)
    proj_matrix = w_proj.reshape(w_proj.shape[0], heads_here * 4 * DH)
    projected = jnp.dot(normed, proj_matrix, preferred_element_type=jnp.float32).reshape(
        rows, heads_here, 4, DH
    )
    gate_rows = jax.nn.silu(projected[:, :, 0]).astype(jnp.bfloat16)
    value_rows = projected[:, :, 1].astype(jnp.bfloat16)
    query_rows = jax.nn.silu(projected[:, :, 2]).astype(jnp.bfloat16)
    key_rows = jax.nn.silu(projected[:, :, 3]).astype(jnp.bfloat16)
    grad_mix = (
        jnp.dot(full_cotangent, w_out.T, preferred_element_type=jnp.float32)
        .astype(jnp.bfloat16)
        .reshape(rows, heads_here, DH)
    )
    row_ids = jnp.arange(rows, dtype=jnp.int32)
    first = jnp.repeat(user_start, TILE)
    length = jnp.repeat(user_length, TILE)
    position = (row_ids // TILE - first) * TILE + row_ids % TILE
    is_live = position < length
    length_wide = length.astype(jnp.float32)
    blocks = 1
    mixer_parts = []
    grad_parts = []
    for head in range(heads_here):
        query_h = query_rows[:, head]
        key_h = key_rows[:, head]
        value_h = value_rows[:, head]
        gate_h = gate_rows[:, head]
        grad_mix_h = grad_mix[:, head]

        def block_step(carry, block):
            grad_key_sum, grad_value_sum = carry
            allowed = (
                (first[:, None] == first[None, :])
                & (position[None, :] <= position[:, None])
                & is_live[:, None]
                & is_live[None, :]
            )
            length_b = length_wide[:, None]
            scores = jnp.dot(query_h, key_h.T, preferred_element_type=jnp.float32) * scale
            weights = jnp.where(allowed, jax.nn.silu(scores) / length_b, 0.0).astype(jnp.bfloat16)
            attended = jnp.dot(weights, value_h, preferred_element_type=jnp.float32)
            inv_attn = lax.rsqrt(jnp.mean(attended * attended, axis=1, keepdims=True) + norm_eps)
            attn_normed = attended * inv_attn
            gate_wide = gate_h.astype(jnp.float32)
            grad_mix_wide = grad_mix_h.astype(jnp.float32)
            mixer_b = (attn_normed * gate_wide).astype(jnp.bfloat16)
            grad_gate_b = grad_mix_wide * attn_normed
            grad_attn_normed = grad_mix_wide * gate_wide
            grad_attended = (
                inv_attn
                * (
                    grad_attn_normed
                    - attn_normed * jnp.mean(grad_attn_normed * attn_normed, axis=1, keepdims=True)
                )
            ).astype(jnp.bfloat16)
            grad_weights = jnp.dot(grad_attended, value_h.T, preferred_element_type=jnp.float32)
            grad_scores = jnp.where(
                allowed, grad_weights / length_b * silu_slope(scores), 0.0
            ).astype(jnp.bfloat16)
            grad_query_b = jnp.dot(grad_scores, key_h, preferred_element_type=jnp.float32) * scale
            grad_key_sum = (
                grad_key_sum
                + jnp.dot(grad_scores.T, query_h, preferred_element_type=jnp.float32) * scale
            )
            grad_value_sum = grad_value_sum + jnp.dot(
                weights.T, grad_attended, preferred_element_type=jnp.float32
            )
            return ((grad_key_sum, grad_value_sum), (mixer_b, grad_gate_b, grad_query_b))

        start_sums = (jnp.zeros((rows, DH), jnp.float32), jnp.zeros((rows, DH), jnp.float32))
        (grad_key, grad_value), stacked = lax.scan(block_step, start_sums, jnp.arange(blocks))
        mixer_h = stacked[0].reshape(rows, DH)
        grad_gate = stacked[1].reshape(rows, DH)
        grad_query = stacked[2].reshape(rows, DH)
        mixer_h, grad_gate, grad_query, grad_key, grad_value = (
            mixer_h,
            grad_gate,
            grad_query,
            grad_key,
            grad_value,
        )
        before_act = projected[:, head]
        mixer_parts.append(mixer_h)
        grad_parts.append(
            jnp.stack(
                [
                    grad_gate * silu_slope(before_act[:, 0]),
                    grad_value,
                    grad_query * silu_slope(before_act[:, 2]),
                    grad_key * silu_slope(before_act[:, 3]),
                ],
                axis=1,
            )
        )
    mixer = jnp.concatenate(mixer_parts, axis=1)
    grad_proj = (
        jnp.stack(grad_parts, axis=1).astype(jnp.bfloat16).reshape(rows, heads_here * 4 * DH)
    )
    own_wide = own_tokens.astype(jnp.float32)
    mix_share = lax.psum_scatter(
        jnp.dot(mixer, w_out, preferred_element_type=jnp.float32),
        "heads",
        scatter_dimension=1,
        tiled=True,
    )
    mixed_own = (own_wide + mix_share).astype(jnp.bfloat16)
    out_term = jnp.dot(full_cotangent.T, mixer, preferred_element_type=jnp.float32)
    proj_term = jnp.dot(normed.T, grad_proj, preferred_element_type=jnp.float32).reshape(
        normed.shape[1], heads_here, 4 * DH
    )
    grad_normed = lax.psum_scatter(
        jnp.dot(grad_proj, proj_matrix.T, preferred_element_type=jnp.float32),
        "heads",
        scatter_dimension=1,
        tiled=True,
    )
    gain_share = lax.dynamic_slice_in_dim(gain, lax.axis_index("heads") * width, width)
    grad_scaled = grad_normed * gain_share[None, :]
    row_totals = lax.psum(jnp.sum(grad_scaled * own_wide, axis=1), "heads")
    input_own = (
        own_cotangent.astype(jnp.float32)
        + inv_rms * grad_scaled
        - own_wide * (inv_rms * inv_rms * inv_rms) * (row_totals / D)[:, None]
    ).astype(jnp.bfloat16)
    norm_factor = 1.0 / math.sqrt(groups * rows)
    proj_cols = heads_here * 4 * DH
    weight_terms = jnp.concatenate(
        [proj_term.reshape(normed.shape[1], proj_cols), out_term], axis=1
    ).reshape(groups, normed.shape[1] // groups, proj_cols + out_term.shape[1])
    weight_sums = jnp.sum(
        lax.all_to_all(weight_terms, "users", split_axis=0, concat_axis=0, tiled=True), axis=0
    )
    proj_sum = weight_sums[:, :proj_cols].reshape(-1, heads_here, 4 * DH)
    out_sum = weight_sums[:, proj_cols:]
    grad_tiles = select_tiles(input_own.reshape(per_owner, TILE, width), back_index, back_valid)
    mixed_tiles = select_tiles(mixed_own.reshape(per_owner, TILE, width), back_index, back_valid)
    home = lax.all_to_all(
        jnp.stack([mixed_tiles, grad_tiles], axis=1),
        "users",
        split_axis=0,
        concat_axis=0,
        tiled=True,
    )
    mixed = jnp.take(home[:, 0], home_index, axis=0).reshape(rows, width)
    input_grad = jnp.take(home[:, 1], home_index, axis=0).reshape(rows, width)
    return (mixed, input_grad, proj_sum * norm_factor, out_sum * norm_factor)


def solution(mesh):
    placed = (
        P("users", "heads"),
        P("users", "heads"),
        P(),
        P(None, "heads", None),
        P("heads", None),
        P(),
        P("users"),
        P("users"),
    )
    return jax.shard_map(
        per_device,
        mesh=mesh,
        in_specs=placed,
        out_specs=(
            P("users", "heads"),
            P("users", "heads"),
            P("users", "heads", None),
            P("users", "heads"),
        ),
        check_vma=False,
    )
```

```python
import math

import jax
import jax.numpy as jnp
from jax import lax
from jax.sharding import PartitionSpec as P

D = 1024
DH = 64
TILE = 128
CAP = 1


norm_eps = 1e-05


def silu_slope(value):
    sigma = jax.nn.sigmoid(value)
    return sigma * (1.0 + value * (1.0 - sigma))


def route_tables(arrival_slot, owner_index, groups, per_owner):
    placed = arrival_slot.reshape(groups, per_owner)
    owners = placed // per_owner
    tile_ids = jnp.arange(per_owner, dtype=jnp.int32)
    same_owner = owners[:, :, None] == owners[:, None, :]
    earlier = tile_ids[None, :] < tile_ids[:, None]
    ranks = jnp.sum((same_owner & earlier[None, :, :]).astype(jnp.int32), axis=2)
    my_owners = lax.dynamic_index_in_dim(owners, owner_index, 0, keepdims=False)
    my_ranks = lax.dynamic_index_in_dim(ranks, owner_index, 0, keepdims=False)
    buffer_ids = jnp.arange(groups * CAP, dtype=jnp.int32)
    peers = buffer_ids // CAP
    turns = buffer_ids % CAP
    chosen = (my_owners[None, :] == peers[:, None]) & (my_ranks[None, :] == turns[:, None])
    send_index = jnp.sum(chosen.astype(jnp.int32) * tile_ids[None, :], axis=1)
    send_valid = jnp.any(chosen, axis=1)
    codes = (jnp.arange(groups, dtype=jnp.int32)[:, None] * CAP + ranks).reshape(-1)
    wanted = owner_index * per_owner + tile_ids
    matches = placed.reshape(-1)[None, :] == wanted[:, None]
    receive_index = jnp.sum(matches.astype(jnp.int32) * codes[None, :], axis=1)
    owner_lines = jnp.repeat(owners, CAP, axis=0)
    rank_lines = jnp.repeat(ranks, CAP, axis=0)
    place_lines = jnp.repeat(placed, CAP, axis=0)
    returning = (owner_lines == owner_index) & (rank_lines == turns[:, None])
    back_index = jnp.sum(
        returning.astype(jnp.int32) * (place_lines - owner_index * per_owner), axis=1
    )
    back_valid = jnp.any(returning, axis=1)
    home_index = my_owners * CAP + my_ranks
    return (send_index, send_valid, receive_index, back_index, back_valid, home_index)


def select_tiles(tiles, index, keep):
    taken = jnp.take(tiles, index, axis=0)
    return jnp.where(keep[:, None, None], taken, jnp.zeros_like(taken))


def per_device(tokens, cotangent, gain, w_proj, w_out, arrival_slot, user_start, user_length):
    groups = lax.axis_size("users")
    owner_index = lax.axis_index("users")
    rows, width = tokens.shape
    per_owner = rows // TILE
    heads_here = w_proj.shape[1]
    scale = DH ** (-0.5)
    send_index, send_valid, receive_index, back_index, back_valid, home_index = route_tables(
        arrival_slot, owner_index, groups, per_owner
    )
    outgoing_tokens = select_tiles(tokens.reshape(per_owner, TILE, width), send_index, send_valid)
    outgoing_grads = select_tiles(cotangent.reshape(per_owner, TILE, width), send_index, send_valid)
    arrived = lax.all_to_all(
        jnp.stack([outgoing_tokens, outgoing_grads], axis=1),
        "users",
        split_axis=0,
        concat_axis=0,
        tiled=True,
    )
    own_both = jnp.take(arrived, receive_index, axis=0)
    own_tokens = own_both[:, 0].reshape(rows, width)
    own_cotangent = own_both[:, 1].reshape(rows, width)
    full_both = lax.all_gather(own_both, "heads", axis=3, tiled=True)
    full_tokens = full_both[:, 0].reshape(rows, -1)
    full_cotangent = full_both[:, 1].reshape(rows, -1)
    tokens_wide = full_tokens.astype(jnp.float32)
    inv_rms = lax.rsqrt(jnp.mean(tokens_wide * tokens_wide, axis=1, keepdims=True) + norm_eps)
    normed = (tokens_wide * inv_rms * gain[None, :]).astype(jnp.bfloat16)
    proj_matrix = w_proj.reshape(w_proj.shape[0], heads_here * 4 * DH)
    projected = jnp.dot(normed, proj_matrix, preferred_element_type=jnp.float32).reshape(
        rows, heads_here, 4, DH
    )
    gate_rows = jax.nn.silu(projected[:, :, 0]).astype(jnp.bfloat16)
    value_rows = projected[:, :, 1].astype(jnp.bfloat16)
    query_rows = jax.nn.silu(projected[:, :, 2]).astype(jnp.bfloat16)
    key_rows = jax.nn.silu(projected[:, :, 3]).astype(jnp.bfloat16)
    grad_mix = (
        jnp.dot(full_cotangent, w_out.T, preferred_element_type=jnp.float32)
        .astype(jnp.bfloat16)
        .reshape(rows, heads_here, DH)
    )
    row_ids = jnp.arange(rows, dtype=jnp.int32)
    first = jnp.repeat(user_start, TILE)
    length = jnp.repeat(user_length, TILE)
    position = (row_ids // TILE - first) * TILE + row_ids % TILE
    is_live = position < length
    length_wide = length.astype(jnp.float32)
    blocks = 1
    mixer_parts = []
    grad_parts = []
    for head in range(heads_here):
        query_h = query_rows[:, head]
        key_h = key_rows[:, head]
        value_h = value_rows[:, head]
        gate_h = gate_rows[:, head]
        grad_mix_h = grad_mix[:, head]

        def block_step(carry, block):
            grad_key_sum, grad_value_sum = carry
            allowed = (
                (first[:, None] == first[None, :])
                & (position[None, :] <= position[:, None])
                & is_live[:, None]
                & is_live[None, :]
            )
            length_b = length_wide[:, None]
            scores = jnp.dot(query_h, key_h.T, preferred_element_type=jnp.float32) * scale
            weights = jnp.where(allowed, jax.nn.silu(scores) / length_b, 0.0).astype(jnp.bfloat16)
            attended = jnp.dot(weights, value_h, preferred_element_type=jnp.float32)
            inv_attn = lax.rsqrt(jnp.mean(attended * attended, axis=1, keepdims=True) + norm_eps)
            attn_normed = attended * inv_attn
            gate_wide = gate_h.astype(jnp.float32)
            grad_mix_wide = grad_mix_h.astype(jnp.float32)
            mixer_b = (attn_normed * gate_wide).astype(jnp.bfloat16)
            grad_gate_b = grad_mix_wide * attn_normed
            grad_attn_normed = grad_mix_wide * gate_wide
            grad_attended = (
                inv_attn
                * (
                    grad_attn_normed
                    - attn_normed * jnp.mean(grad_attn_normed * attn_normed, axis=1, keepdims=True)
                )
            ).astype(jnp.bfloat16)
            grad_weights = jnp.dot(grad_attended, value_h.T, preferred_element_type=jnp.float32)
            grad_scores = jnp.where(
                allowed, grad_weights / length_b * silu_slope(scores), 0.0
            ).astype(jnp.bfloat16)
            grad_query_b = jnp.dot(grad_scores, key_h, preferred_element_type=jnp.float32) * scale
            grad_key_sum = (
                grad_key_sum
                + jnp.dot(grad_scores.T, query_h, preferred_element_type=jnp.float32) * scale
            )
            grad_value_sum = grad_value_sum + jnp.dot(
                weights.T, grad_attended, preferred_element_type=jnp.float32
            )
            return ((grad_key_sum, grad_value_sum), (mixer_b, grad_gate_b, grad_query_b))

        start_sums = (jnp.zeros((rows, DH), jnp.float32), jnp.zeros((rows, DH), jnp.float32))
        (grad_key, grad_value), stacked = lax.scan(block_step, start_sums, jnp.arange(blocks))
        mixer_h = stacked[0].reshape(rows, DH)
        grad_gate = stacked[1].reshape(rows, DH)
        grad_query = stacked[2].reshape(rows, DH)
        mixer_h, grad_gate, grad_query, grad_key, grad_value = (
            mixer_h,
            grad_gate,
            grad_query,
            grad_key,
            grad_value,
        )
        before_act = projected[:, head]
        mixer_parts.append(mixer_h)
        grad_parts.append(
            jnp.stack(
                [
                    grad_gate * silu_slope(before_act[:, 0]),
                    grad_value,
                    grad_query * silu_slope(before_act[:, 2]),
                    grad_key * silu_slope(before_act[:, 3]),
                ],
                axis=1,
            )
        )
    mixer = jnp.concatenate(mixer_parts, axis=1)
    grad_proj = (
        jnp.stack(grad_parts, axis=1).astype(jnp.bfloat16).reshape(rows, heads_here * 4 * DH)
    )
    own_wide = own_tokens.astype(jnp.float32)
    mix_share = lax.psum_scatter(
        jnp.dot(mixer, w_out, preferred_element_type=jnp.float32),
        "heads",
        scatter_dimension=1,
        tiled=True,
    )
    mixed_own = (own_wide + mix_share).astype(jnp.bfloat16)
    out_term = jnp.dot(full_cotangent.T, mixer, preferred_element_type=jnp.float32)
    proj_term = jnp.dot(normed.T, grad_proj, preferred_element_type=jnp.float32).reshape(
        normed.shape[1], heads_here, 4 * DH
    )
    heads_count = lax.axis_size("heads")
    normed_partial = jnp.dot(grad_proj, proj_matrix.T, preferred_element_type=jnp.float32)
    partial_totals = jnp.sum(normed_partial * (tokens_wide * gain[None, :]), axis=1)
    extra = -(-rows // width)
    partial_totals = jnp.pad(partial_totals, (0, extra * width - rows)).reshape(1, extra, width)
    reduced = lax.psum_scatter(
        jnp.concatenate(
            [
                normed_partial.reshape(rows, heads_count, width).transpose(1, 0, 2),
                jnp.broadcast_to(partial_totals, (heads_count, extra, width)),
            ],
            axis=1,
        ),
        "heads",
        scatter_dimension=0,
        tiled=True,
    )
    grad_normed = reduced[0, :rows]
    row_totals = reduced[0, rows:].reshape(-1)[:rows]
    gain_share = lax.dynamic_slice_in_dim(gain, lax.axis_index("heads") * width, width)
    grad_scaled = grad_normed * gain_share[None, :]
    input_own = (
        own_cotangent.astype(jnp.float32)
        + inv_rms * grad_scaled
        - own_wide * (inv_rms * inv_rms * inv_rms) * (row_totals / D)[:, None]
    ).astype(jnp.bfloat16)
    norm_factor = 1.0 / math.sqrt(groups * rows)
    proj_cols = heads_here * 4 * DH
    weight_terms = jnp.concatenate(
        [proj_term.reshape(normed.shape[1], proj_cols), out_term], axis=1
    ).reshape(groups, normed.shape[1] // groups, proj_cols + out_term.shape[1])
    weight_sums = jnp.sum(
        lax.all_to_all(weight_terms, "users", split_axis=0, concat_axis=0, tiled=True), axis=0
    )
    proj_sum = weight_sums[:, :proj_cols].reshape(-1, heads_here, 4 * DH)
    out_sum = weight_sums[:, proj_cols:]
    grad_tiles = select_tiles(input_own.reshape(per_owner, TILE, width), back_index, back_valid)
    mixed_tiles = select_tiles(mixed_own.reshape(per_owner, TILE, width), back_index, back_valid)
    home = lax.all_to_all(
        jnp.stack([mixed_tiles, grad_tiles], axis=1),
        "users",
        split_axis=0,
        concat_axis=0,
        tiled=True,
    )
    mixed = jnp.take(home[:, 0], home_index, axis=0).reshape(rows, width)
    input_grad = jnp.take(home[:, 1], home_index, axis=0).reshape(rows, width)
    return (mixed, input_grad, proj_sum * norm_factor, out_sum * norm_factor)


def solution(mesh):
    placed = (
        P("users", "heads"),
        P("users", "heads"),
        P(),
        P(None, "heads", None),
        P("heads", None),
        P(),
        P("users"),
        P("users"),
    )
    return jax.shard_map(
        per_device,
        mesh=mesh,
        in_specs=placed,
        out_specs=(
            P("users", "heads"),
            P("users", "heads"),
            P("users", "heads", None),
            P("users", "heads"),
        ),
        check_vma=False,
    )
```

```python
import math

import jax
import jax.numpy as jnp
from jax import lax
from jax.sharding import PartitionSpec as P

D = 1024
DH = 64
TILE = 128
CAP = 1


norm_eps = 1e-05


def silu_slope(value):
    sigma = jax.nn.sigmoid(value)
    return sigma * (1.0 + value * (1.0 - sigma))


def route_tables(arrival_slot, owner_index, groups, per_owner):
    placed = arrival_slot.reshape(groups, per_owner)
    owners = placed // per_owner
    tile_ids = jnp.arange(per_owner, dtype=jnp.int32)
    same_owner = owners[:, :, None] == owners[:, None, :]
    earlier = tile_ids[None, :] < tile_ids[:, None]
    ranks = jnp.sum((same_owner & earlier[None, :, :]).astype(jnp.int32), axis=2)
    my_owners = lax.dynamic_index_in_dim(owners, owner_index, 0, keepdims=False)
    my_ranks = lax.dynamic_index_in_dim(ranks, owner_index, 0, keepdims=False)
    buffer_ids = jnp.arange(groups * CAP, dtype=jnp.int32)
    peers = buffer_ids // CAP
    turns = buffer_ids % CAP
    chosen = (my_owners[None, :] == peers[:, None]) & (my_ranks[None, :] == turns[:, None])
    send_index = jnp.sum(chosen.astype(jnp.int32) * tile_ids[None, :], axis=1)
    send_valid = jnp.any(chosen, axis=1)
    codes = (jnp.arange(groups, dtype=jnp.int32)[:, None] * CAP + ranks).reshape(-1)
    wanted = owner_index * per_owner + tile_ids
    matches = placed.reshape(-1)[None, :] == wanted[:, None]
    receive_index = jnp.sum(matches.astype(jnp.int32) * codes[None, :], axis=1)
    owner_lines = jnp.repeat(owners, CAP, axis=0)
    rank_lines = jnp.repeat(ranks, CAP, axis=0)
    place_lines = jnp.repeat(placed, CAP, axis=0)
    returning = (owner_lines == owner_index) & (rank_lines == turns[:, None])
    back_index = jnp.sum(
        returning.astype(jnp.int32) * (place_lines - owner_index * per_owner), axis=1
    )
    back_valid = jnp.any(returning, axis=1)
    home_index = my_owners * CAP + my_ranks
    return (send_index, send_valid, receive_index, back_index, back_valid, home_index)


def select_tiles(tiles, index, keep):
    taken = jnp.take(tiles, index, axis=0)
    return jnp.where(keep[:, None, None], taken, jnp.zeros_like(taken))


def per_device(tokens, cotangent, gain, w_proj, w_out, arrival_slot, user_start, user_length):
    groups = lax.axis_size("users")
    owner_index = lax.axis_index("users")
    rows, width = tokens.shape
    per_owner = rows // TILE
    heads_here = w_proj.shape[1]
    scale = DH ** (-0.5)
    send_index, send_valid, receive_index, back_index, back_valid, home_index = route_tables(
        arrival_slot, owner_index, groups, per_owner
    )
    outgoing_tokens = select_tiles(tokens.reshape(per_owner, TILE, width), send_index, send_valid)
    outgoing_grads = select_tiles(cotangent.reshape(per_owner, TILE, width), send_index, send_valid)
    arrived = lax.all_to_all(
        jnp.stack([outgoing_tokens, outgoing_grads], axis=1),
        "users",
        split_axis=0,
        concat_axis=0,
        tiled=True,
    )
    own_both = jnp.take(arrived, receive_index, axis=0)
    own_tokens = own_both[:, 0].reshape(rows, width)
    own_cotangent = own_both[:, 1].reshape(rows, width)
    full_both = lax.all_gather(own_both, "heads", axis=3, tiled=True)
    full_tokens = full_both[:, 0].reshape(rows, -1)
    full_cotangent = full_both[:, 1].reshape(rows, -1)
    tokens_wide = full_tokens.astype(jnp.float32)
    inv_rms = lax.rsqrt(jnp.mean(tokens_wide * tokens_wide, axis=1, keepdims=True) + norm_eps)
    normed = (tokens_wide * inv_rms * gain[None, :]).astype(jnp.bfloat16)
    proj_matrix = w_proj.reshape(w_proj.shape[0], heads_here * 4 * DH)
    projected = jnp.dot(normed, proj_matrix, preferred_element_type=jnp.float32).reshape(
        rows, heads_here, 4, DH
    )
    gate_rows = jax.nn.silu(projected[:, :, 0]).astype(jnp.bfloat16)
    value_rows = projected[:, :, 1].astype(jnp.bfloat16)
    query_rows = jax.nn.silu(projected[:, :, 2]).astype(jnp.bfloat16)
    key_rows = jax.nn.silu(projected[:, :, 3]).astype(jnp.bfloat16)
    grad_mix = (
        jnp.dot(full_cotangent, w_out.T, preferred_element_type=jnp.float32)
        .astype(jnp.bfloat16)
        .reshape(rows, heads_here, DH)
    )
    row_ids = jnp.arange(rows, dtype=jnp.int32)
    first = jnp.repeat(user_start, TILE)
    length = jnp.repeat(user_length, TILE)
    position = (row_ids // TILE - first) * TILE + row_ids % TILE
    is_live = position < length
    length_wide = length.astype(jnp.float32)
    blocks = 1
    mixer_parts = []
    grad_parts = []
    for head in range(heads_here):
        query_h = query_rows[:, head]
        key_h = key_rows[:, head]
        value_h = value_rows[:, head]
        gate_h = gate_rows[:, head]
        grad_mix_h = grad_mix[:, head]

        def block_step(carry, block):
            grad_key_sum, grad_value_sum = carry
            allowed = (
                (first[:, None] == first[None, :])
                & (position[None, :] <= position[:, None])
                & is_live[:, None]
                & is_live[None, :]
            )
            length_b = length_wide[:, None]
            scores = jnp.dot(query_h, key_h.T, preferred_element_type=jnp.float32) * scale
            weights = jnp.where(allowed, jax.nn.silu(scores) / length_b, 0.0).astype(jnp.bfloat16)
            attended = jnp.dot(weights, value_h, preferred_element_type=jnp.float32)
            inv_attn = lax.rsqrt(jnp.mean(attended * attended, axis=1, keepdims=True) + norm_eps)
            attn_normed = attended * inv_attn
            gate_wide = gate_h.astype(jnp.float32)
            grad_mix_wide = grad_mix_h.astype(jnp.float32)
            mixer_b = (attn_normed * gate_wide).astype(jnp.bfloat16)
            grad_gate_b = grad_mix_wide * attn_normed
            grad_attn_normed = grad_mix_wide * gate_wide
            grad_attended = (
                inv_attn
                * (
                    grad_attn_normed
                    - attn_normed * jnp.mean(grad_attn_normed * attn_normed, axis=1, keepdims=True)
                )
            ).astype(jnp.bfloat16)
            grad_weights = jnp.dot(grad_attended, value_h.T, preferred_element_type=jnp.float32)
            grad_scores = jnp.where(
                allowed, grad_weights / length_b * silu_slope(scores), 0.0
            ).astype(jnp.bfloat16)
            grad_query_b = jnp.dot(grad_scores, key_h, preferred_element_type=jnp.float32) * scale
            grad_key_sum = (
                grad_key_sum
                + jnp.dot(grad_scores.T, query_h, preferred_element_type=jnp.float32) * scale
            )
            grad_value_sum = grad_value_sum + jnp.dot(
                weights.T, grad_attended, preferred_element_type=jnp.float32
            )
            return ((grad_key_sum, grad_value_sum), (mixer_b, grad_gate_b, grad_query_b))

        start_sums = (jnp.zeros((rows, DH), jnp.float32), jnp.zeros((rows, DH), jnp.float32))
        (grad_key, grad_value), stacked = lax.scan(block_step, start_sums, jnp.arange(blocks))
        mixer_h = stacked[0].reshape(rows, DH)
        grad_gate = stacked[1].reshape(rows, DH)
        grad_query = stacked[2].reshape(rows, DH)
        mixer_h, grad_gate, grad_query, grad_key, grad_value = (
            mixer_h,
            grad_gate,
            grad_query,
            grad_key,
            grad_value,
        )
        before_act = projected[:, head]
        mixer_parts.append(mixer_h)
        grad_parts.append(
            jnp.stack(
                [
                    grad_gate * silu_slope(before_act[:, 0]),
                    grad_value,
                    grad_query * silu_slope(before_act[:, 2]),
                    grad_key * silu_slope(before_act[:, 3]),
                ],
                axis=1,
            )
        )
    mixer = jnp.concatenate(mixer_parts, axis=1)
    grad_proj = (
        jnp.stack(grad_parts, axis=1).astype(jnp.bfloat16).reshape(rows, heads_here * 4 * DH)
    )
    own_wide = own_tokens.astype(jnp.float32)
    mix_share = lax.psum_scatter(
        jnp.dot(mixer, w_out, preferred_element_type=jnp.float32),
        "heads",
        scatter_dimension=1,
        tiled=True,
    )
    mixed_own = (own_wide + mix_share).astype(jnp.bfloat16)
    out_term = jnp.dot(full_cotangent.T, mixer, preferred_element_type=jnp.float32)
    proj_term = jnp.dot(normed.T, grad_proj, preferred_element_type=jnp.float32).reshape(
        normed.shape[1], heads_here, 4 * DH
    )
    heads_count = lax.axis_size("heads")
    normed_partial = jnp.dot(grad_proj, proj_matrix.T, preferred_element_type=jnp.float32)
    partial_totals = jnp.sum(normed_partial * (tokens_wide * gain[None, :]), axis=1)
    extra = -(-rows // width)
    partial_totals = jnp.pad(partial_totals, (0, extra * width - rows)).reshape(1, extra, width)
    reduced = lax.psum_scatter(
        jnp.concatenate(
            [
                normed_partial.reshape(rows, heads_count, width).transpose(1, 0, 2),
                jnp.broadcast_to(partial_totals, (heads_count, extra, width)),
            ],
            axis=1,
        ).astype(jnp.bfloat16),
        "heads",
        scatter_dimension=0,
        tiled=True,
    ).astype(jnp.float32)
    grad_normed = reduced[0, :rows]
    row_totals = reduced[0, rows:].reshape(-1)[:rows]
    gain_share = lax.dynamic_slice_in_dim(gain, lax.axis_index("heads") * width, width)
    grad_scaled = grad_normed * gain_share[None, :]
    input_own = (
        own_cotangent.astype(jnp.float32)
        + inv_rms * grad_scaled
        - own_wide * (inv_rms * inv_rms * inv_rms) * (row_totals / D)[:, None]
    ).astype(jnp.bfloat16)
    norm_factor = 1.0 / math.sqrt(groups * rows)
    proj_cols = heads_here * 4 * DH
    weight_terms = jnp.concatenate(
        [proj_term.reshape(normed.shape[1], proj_cols), out_term], axis=1
    ).reshape(groups, normed.shape[1] // groups, proj_cols + out_term.shape[1])
    weight_sums = jnp.sum(
        lax.all_to_all(
            weight_terms.astype(jnp.bfloat16), "users", split_axis=0, concat_axis=0, tiled=True
        ).astype(jnp.float32),
        axis=0,
    )
    proj_sum = weight_sums[:, :proj_cols].reshape(-1, heads_here, 4 * DH)
    out_sum = weight_sums[:, proj_cols:]
    grad_tiles = select_tiles(input_own.reshape(per_owner, TILE, width), back_index, back_valid)
    mixed_tiles = select_tiles(mixed_own.reshape(per_owner, TILE, width), back_index, back_valid)
    home = lax.all_to_all(
        jnp.stack([mixed_tiles, grad_tiles], axis=1),
        "users",
        split_axis=0,
        concat_axis=0,
        tiled=True,
    )
    mixed = jnp.take(home[:, 0], home_index, axis=0).reshape(rows, width)
    input_grad = jnp.take(home[:, 1], home_index, axis=0).reshape(rows, width)
    return (mixed, input_grad, proj_sum * norm_factor, out_sum * norm_factor)


def solution(mesh):
    placed = (
        P("users", "heads"),
        P("users", "heads"),
        P(),
        P(None, "heads", None),
        P("heads", None),
        P(),
        P("users"),
        P("users"),
    )
    return jax.shard_map(
        per_device,
        mesh=mesh,
        in_specs=placed,
        out_specs=(
            P("users", "heads"),
            P("users", "heads"),
            P("users", "heads", None),
            P("users", "heads"),
        ),
        check_vma=False,
    )
```

```python
import math

import jax
import jax.numpy as jnp
from jax import lax
from jax.sharding import PartitionSpec as P

D = 1024
DH = 64
TILE = 128
CAP = 1


norm_eps = 1e-05


def silu_slope(value):
    sigma = jax.nn.sigmoid(value)
    return sigma * (1.0 + value * (1.0 - sigma))


def route_tables(arrival_slot, owner_index, groups, per_owner):
    placed = arrival_slot.reshape(groups, per_owner)
    owners = placed // per_owner
    tile_ids = jnp.arange(per_owner, dtype=jnp.int32)
    same_owner = owners[:, :, None] == owners[:, None, :]
    earlier = tile_ids[None, :] < tile_ids[:, None]
    ranks = jnp.sum((same_owner & earlier[None, :, :]).astype(jnp.int32), axis=2)
    my_owners = lax.dynamic_index_in_dim(owners, owner_index, 0, keepdims=False)
    my_ranks = lax.dynamic_index_in_dim(ranks, owner_index, 0, keepdims=False)
    buffer_ids = jnp.arange(groups * CAP, dtype=jnp.int32)
    peers = buffer_ids // CAP
    turns = buffer_ids % CAP
    chosen = (my_owners[None, :] == peers[:, None]) & (my_ranks[None, :] == turns[:, None])
    send_index = jnp.sum(chosen.astype(jnp.int32) * tile_ids[None, :], axis=1)
    send_valid = jnp.any(chosen, axis=1)
    codes = (jnp.arange(groups, dtype=jnp.int32)[:, None] * CAP + ranks).reshape(-1)
    wanted = owner_index * per_owner + tile_ids
    matches = placed.reshape(-1)[None, :] == wanted[:, None]
    receive_index = jnp.sum(matches.astype(jnp.int32) * codes[None, :], axis=1)
    owner_lines = jnp.repeat(owners, CAP, axis=0)
    rank_lines = jnp.repeat(ranks, CAP, axis=0)
    place_lines = jnp.repeat(placed, CAP, axis=0)
    returning = (owner_lines == owner_index) & (rank_lines == turns[:, None])
    back_index = jnp.sum(
        returning.astype(jnp.int32) * (place_lines - owner_index * per_owner), axis=1
    )
    back_valid = jnp.any(returning, axis=1)
    home_index = my_owners * CAP + my_ranks
    return (send_index, send_valid, receive_index, back_index, back_valid, home_index)


def select_tiles(tiles, index, keep):
    taken = jnp.take(tiles, index, axis=0)
    return jnp.where(keep[:, None, None], taken, jnp.zeros_like(taken))


def per_device(tokens, cotangent, gain, w_proj, w_out, arrival_slot, user_start, user_length):
    groups = lax.axis_size("users")
    owner_index = lax.axis_index("users")
    rows, width = tokens.shape
    per_owner = rows // TILE
    heads_here = w_proj.shape[1]
    scale = DH ** (-0.5)
    send_index, send_valid, receive_index, back_index, back_valid, home_index = route_tables(
        arrival_slot, owner_index, groups, per_owner
    )
    outgoing_tokens = select_tiles(tokens.reshape(per_owner, TILE, width), send_index, send_valid)
    outgoing_grads = select_tiles(cotangent.reshape(per_owner, TILE, width), send_index, send_valid)
    arrived = lax.all_to_all(
        jnp.stack([outgoing_tokens, outgoing_grads], axis=1),
        "users",
        split_axis=0,
        concat_axis=0,
        tiled=True,
    )
    own_both = jnp.take(arrived, receive_index, axis=0)
    own_tokens = own_both[:, 0].reshape(rows, width)
    own_cotangent = own_both[:, 1].reshape(rows, width)
    full_both = lax.all_gather(own_both, "heads", axis=3, tiled=True)
    full_tokens = full_both[:, 0].reshape(rows, -1)
    full_cotangent = full_both[:, 1].reshape(rows, -1)
    tokens_wide = full_tokens.astype(jnp.float32)
    inv_rms = lax.rsqrt(jnp.mean(tokens_wide * tokens_wide, axis=1, keepdims=True) + norm_eps)
    normed = (tokens_wide * inv_rms * gain[None, :]).astype(jnp.bfloat16)
    proj_matrix = w_proj.reshape(w_proj.shape[0], heads_here * 4 * DH)
    projected = jnp.dot(normed, proj_matrix, preferred_element_type=jnp.float32).reshape(
        rows, heads_here, 4, DH
    )
    gate_rows = jax.nn.silu(projected[:, :, 0]).astype(jnp.bfloat16)
    value_rows = projected[:, :, 1].astype(jnp.bfloat16)
    query_rows = jax.nn.silu(projected[:, :, 2]).astype(jnp.bfloat16)
    key_rows = jax.nn.silu(projected[:, :, 3]).astype(jnp.bfloat16)
    grad_mix = (
        jnp.dot(full_cotangent, w_out.T, preferred_element_type=jnp.float32)
        .astype(jnp.bfloat16)
        .reshape(rows, heads_here, DH)
    )
    row_ids = jnp.arange(rows, dtype=jnp.int32)
    first = jnp.repeat(user_start, TILE)
    length = jnp.repeat(user_length, TILE)
    position = (row_ids // TILE - first) * TILE + row_ids % TILE
    is_live = position < length
    length_wide = length.astype(jnp.float32)
    blocks = 1
    mixer_parts = []
    grad_parts = []
    for head in range(heads_here):
        query_h = query_rows[:, head]
        key_h = key_rows[:, head]
        value_h = value_rows[:, head]
        gate_h = gate_rows[:, head]
        grad_mix_h = grad_mix[:, head]

        def block_step(carry, block):
            grad_key_sum, grad_value_sum = carry
            allowed = (
                (first[:, None] == first[None, :])
                & (position[None, :] <= position[:, None])
                & is_live[:, None]
                & is_live[None, :]
            )
            length_b = length_wide[:, None]
            scores = jnp.dot(query_h, key_h.T, preferred_element_type=jnp.float32) * scale
            weights = jnp.where(allowed, jax.nn.silu(scores) / length_b, 0.0).astype(jnp.bfloat16)
            attended = jnp.dot(weights, value_h, preferred_element_type=jnp.float32)
            inv_attn = lax.rsqrt(jnp.mean(attended * attended, axis=1, keepdims=True) + norm_eps)
            attn_normed = attended * inv_attn
            gate_wide = gate_h.astype(jnp.float32)
            grad_mix_wide = grad_mix_h.astype(jnp.float32)
            mixer_b = (attn_normed * gate_wide).astype(jnp.bfloat16)
            grad_gate_b = grad_mix_wide * attn_normed
            grad_attn_normed = grad_mix_wide * gate_wide
            grad_attended = (
                inv_attn
                * (
                    grad_attn_normed
                    - attn_normed * jnp.mean(grad_attn_normed * attn_normed, axis=1, keepdims=True)
                )
            ).astype(jnp.bfloat16)
            grad_weights = jnp.dot(grad_attended, value_h.T, preferred_element_type=jnp.float32)
            grad_scores = jnp.where(
                allowed, grad_weights / length_b * silu_slope(scores), 0.0
            ).astype(jnp.bfloat16)
            grad_query_b = jnp.dot(grad_scores, key_h, preferred_element_type=jnp.float32) * scale
            grad_key_sum = (
                grad_key_sum
                + jnp.dot(grad_scores.T, query_h, preferred_element_type=jnp.float32) * scale
            )
            grad_value_sum = grad_value_sum + jnp.dot(
                weights.T, grad_attended, preferred_element_type=jnp.float32
            )
            return ((grad_key_sum, grad_value_sum), (mixer_b, grad_gate_b, grad_query_b))

        start_sums = (jnp.zeros((rows, DH), jnp.float32), jnp.zeros((rows, DH), jnp.float32))
        (grad_key, grad_value), stacked = lax.scan(block_step, start_sums, jnp.arange(blocks))
        mixer_h = stacked[0].reshape(rows, DH)
        grad_gate = stacked[1].reshape(rows, DH)
        grad_query = stacked[2].reshape(rows, DH)
        mixer_h, grad_gate, grad_query, grad_key, grad_value = (
            mixer_h,
            grad_gate,
            grad_query,
            grad_key,
            grad_value,
        )
        before_act = projected[:, head]
        mixer_parts.append(mixer_h)
        grad_parts.append(
            jnp.stack(
                [
                    grad_gate * silu_slope(before_act[:, 0]),
                    grad_value,
                    grad_query * silu_slope(before_act[:, 2]),
                    grad_key * silu_slope(before_act[:, 3]),
                ],
                axis=1,
            )
        )
    mixer = jnp.concatenate(mixer_parts, axis=1)
    grad_proj = (
        jnp.stack(grad_parts, axis=1).astype(jnp.bfloat16).reshape(rows, heads_here * 4 * DH)
    )
    own_wide = own_tokens.astype(jnp.float32)
    mix_partial = jnp.dot(mixer, w_out, preferred_element_type=jnp.float32)
    out_term = jnp.dot(full_cotangent.T, mixer, preferred_element_type=jnp.float32)
    proj_term = jnp.dot(normed.T, grad_proj, preferred_element_type=jnp.float32).reshape(
        normed.shape[1], heads_here, 4 * DH
    )
    heads_count = lax.axis_size("heads")
    normed_partial = jnp.dot(grad_proj, proj_matrix.T, preferred_element_type=jnp.float32)
    partial_totals = jnp.sum(normed_partial * (tokens_wide * gain[None, :]), axis=1)
    extra = -(-rows // width)
    partial_totals = jnp.pad(partial_totals, (0, extra * width - rows)).reshape(1, extra, width)
    reduced = lax.psum_scatter(
        jnp.concatenate(
            [
                normed_partial.reshape(rows, heads_count, width).transpose(1, 0, 2),
                jnp.broadcast_to(partial_totals, (heads_count, extra, width)),
                mix_partial.reshape(rows, heads_count, width).transpose(1, 0, 2),
            ],
            axis=1,
        ).astype(jnp.bfloat16),
        "heads",
        scatter_dimension=0,
        tiled=True,
    ).astype(jnp.float32)
    grad_normed = reduced[0, :rows]
    row_totals = reduced[0, rows : rows + extra].reshape(-1)[:rows]
    mixed_own = (own_wide + reduced[0, rows + extra :]).astype(jnp.bfloat16)
    gain_share = lax.dynamic_slice_in_dim(gain, lax.axis_index("heads") * width, width)
    grad_scaled = grad_normed * gain_share[None, :]
    input_own = (
        own_cotangent.astype(jnp.float32)
        + inv_rms * grad_scaled
        - own_wide * (inv_rms * inv_rms * inv_rms) * (row_totals / D)[:, None]
    ).astype(jnp.bfloat16)
    norm_factor = 1.0 / math.sqrt(groups * rows)
    proj_cols = heads_here * 4 * DH
    weight_terms = jnp.concatenate(
        [proj_term.reshape(normed.shape[1], proj_cols), out_term], axis=1
    ).reshape(groups, normed.shape[1] // groups, proj_cols + out_term.shape[1])
    weight_sums = jnp.sum(
        lax.all_to_all(
            weight_terms.astype(jnp.bfloat16), "users", split_axis=0, concat_axis=0, tiled=True
        ).astype(jnp.float32),
        axis=0,
    )
    proj_sum = weight_sums[:, :proj_cols].reshape(-1, heads_here, 4 * DH)
    out_sum = weight_sums[:, proj_cols:]
    grad_tiles = select_tiles(input_own.reshape(per_owner, TILE, width), back_index, back_valid)
    mixed_tiles = select_tiles(mixed_own.reshape(per_owner, TILE, width), back_index, back_valid)
    home = lax.all_to_all(
        jnp.stack([mixed_tiles, grad_tiles], axis=1),
        "users",
        split_axis=0,
        concat_axis=0,
        tiled=True,
    )
    mixed = jnp.take(home[:, 0], home_index, axis=0).reshape(rows, width)
    input_grad = jnp.take(home[:, 1], home_index, axis=0).reshape(rows, width)
    return (mixed, input_grad, proj_sum * norm_factor, out_sum * norm_factor)


def solution(mesh):
    placed = (
        P("users", "heads"),
        P("users", "heads"),
        P(),
        P(None, "heads", None),
        P("heads", None),
        P(),
        P("users"),
        P("users"),
    )
    return jax.shard_map(
        per_device,
        mesh=mesh,
        in_specs=placed,
        out_specs=(
            P("users", "heads"),
            P("users", "heads"),
            P("users", "heads", None),
            P("users", "heads"),
        ),
        check_vma=False,
    )
```

```python
import math

import jax
import jax.numpy as jnp
from jax import lax
from jax.sharding import PartitionSpec as P

D = 1024
DH = 64
TILE = 128
CAP = 1


norm_eps = 1e-05


def silu_slope(value):
    sigma = jax.nn.sigmoid(value)
    return sigma * (1.0 + value * (1.0 - sigma))


def route_tables(arrival_slot, owner_index, groups, per_owner):
    placed = arrival_slot.reshape(groups, per_owner)
    owners = placed // per_owner
    tile_ids = jnp.arange(per_owner, dtype=jnp.int32)
    same_owner = owners[:, :, None] == owners[:, None, :]
    earlier = tile_ids[None, :] < tile_ids[:, None]
    ranks = jnp.sum((same_owner & earlier[None, :, :]).astype(jnp.int32), axis=2)
    my_owners = lax.dynamic_index_in_dim(owners, owner_index, 0, keepdims=False)
    my_ranks = lax.dynamic_index_in_dim(ranks, owner_index, 0, keepdims=False)
    buffer_ids = jnp.arange(groups * CAP, dtype=jnp.int32)
    peers = buffer_ids // CAP
    turns = buffer_ids % CAP
    chosen = (my_owners[None, :] == peers[:, None]) & (my_ranks[None, :] == turns[:, None])
    send_index = jnp.sum(chosen.astype(jnp.int32) * tile_ids[None, :], axis=1)
    send_valid = jnp.any(chosen, axis=1)
    codes = (jnp.arange(groups, dtype=jnp.int32)[:, None] * CAP + ranks).reshape(-1)
    wanted = owner_index * per_owner + tile_ids
    matches = placed.reshape(-1)[None, :] == wanted[:, None]
    receive_index = jnp.sum(matches.astype(jnp.int32) * codes[None, :], axis=1)
    owner_lines = jnp.repeat(owners, CAP, axis=0)
    rank_lines = jnp.repeat(ranks, CAP, axis=0)
    place_lines = jnp.repeat(placed, CAP, axis=0)
    returning = (owner_lines == owner_index) & (rank_lines == turns[:, None])
    back_index = jnp.sum(
        returning.astype(jnp.int32) * (place_lines - owner_index * per_owner), axis=1
    )
    back_valid = jnp.any(returning, axis=1)
    home_index = my_owners * CAP + my_ranks
    return (send_index, send_valid, receive_index, back_index, back_valid, home_index)


def select_tiles(tiles, index, keep):
    taken = jnp.take(tiles, index, axis=0)
    return jnp.where(keep[:, None, None], taken, jnp.zeros_like(taken))


def per_device(tokens, cotangent, gain, w_proj, w_out, arrival_slot, user_start, user_length):
    groups = lax.axis_size("users")
    owner_index = lax.axis_index("users")
    rows, width = tokens.shape
    per_owner = rows // TILE
    heads_here = w_proj.shape[1]
    scale = DH ** (-0.5)
    send_index, send_valid, receive_index, back_index, back_valid, home_index = route_tables(
        arrival_slot, owner_index, groups, per_owner
    )
    outgoing_tokens = select_tiles(tokens.reshape(per_owner, TILE, width), send_index, send_valid)
    outgoing_grads = select_tiles(cotangent.reshape(per_owner, TILE, width), send_index, send_valid)
    arrived = lax.all_to_all(
        jnp.stack([outgoing_tokens, outgoing_grads], axis=1),
        "users",
        split_axis=0,
        concat_axis=0,
        tiled=True,
    )
    own_both = jnp.take(arrived, receive_index, axis=0)
    own_tokens = own_both[:, 0].reshape(rows, width)
    own_cotangent = own_both[:, 1].reshape(rows, width)
    full_tokens = lax.all_gather(own_both[:, 0], "heads", axis=2, tiled=True).reshape(rows, -1)
    full_cotangent = lax.all_gather(own_both[:, 1], "heads", axis=2, tiled=True).reshape(rows, -1)
    tokens_wide = full_tokens.astype(jnp.float32)
    inv_rms = lax.rsqrt(jnp.mean(tokens_wide * tokens_wide, axis=1, keepdims=True) + norm_eps)
    normed = (tokens_wide * inv_rms * gain[None, :]).astype(jnp.bfloat16)
    proj_matrix = w_proj.reshape(w_proj.shape[0], heads_here * 4 * DH)
    projected = jnp.dot(normed, proj_matrix, preferred_element_type=jnp.float32).reshape(
        rows, heads_here, 4, DH
    )
    gate_rows = jax.nn.silu(projected[:, :, 0]).astype(jnp.bfloat16)
    value_rows = projected[:, :, 1].astype(jnp.bfloat16)
    query_rows = jax.nn.silu(projected[:, :, 2]).astype(jnp.bfloat16)
    key_rows = jax.nn.silu(projected[:, :, 3]).astype(jnp.bfloat16)
    grad_mix = (
        jnp.dot(full_cotangent, w_out.T, preferred_element_type=jnp.float32)
        .astype(jnp.bfloat16)
        .reshape(rows, heads_here, DH)
    )
    row_ids = jnp.arange(rows, dtype=jnp.int32)
    first = jnp.repeat(user_start, TILE)
    length = jnp.repeat(user_length, TILE)
    position = (row_ids // TILE - first) * TILE + row_ids % TILE
    is_live = position < length
    length_wide = length.astype(jnp.float32)
    blocks = 1
    mixer_parts = []
    grad_parts = []
    for head in range(heads_here):
        query_h = query_rows[:, head]
        key_h = key_rows[:, head]
        value_h = value_rows[:, head]
        gate_h = gate_rows[:, head]
        grad_mix_h = grad_mix[:, head]

        def block_step(carry, block):
            grad_key_sum, grad_value_sum = carry
            allowed = (
                (first[:, None] == first[None, :])
                & (position[None, :] <= position[:, None])
                & is_live[:, None]
                & is_live[None, :]
            )
            length_b = length_wide[:, None]
            scores = jnp.dot(query_h, key_h.T, preferred_element_type=jnp.float32) * scale
            weights = jnp.where(allowed, jax.nn.silu(scores) / length_b, 0.0).astype(jnp.bfloat16)
            attended = jnp.dot(weights, value_h, preferred_element_type=jnp.float32)
            inv_attn = lax.rsqrt(jnp.mean(attended * attended, axis=1, keepdims=True) + norm_eps)
            attn_normed = attended * inv_attn
            gate_wide = gate_h.astype(jnp.float32)
            grad_mix_wide = grad_mix_h.astype(jnp.float32)
            mixer_b = (attn_normed * gate_wide).astype(jnp.bfloat16)
            grad_gate_b = grad_mix_wide * attn_normed
            grad_attn_normed = grad_mix_wide * gate_wide
            grad_attended = (
                inv_attn
                * (
                    grad_attn_normed
                    - attn_normed * jnp.mean(grad_attn_normed * attn_normed, axis=1, keepdims=True)
                )
            ).astype(jnp.bfloat16)
            grad_weights = jnp.dot(grad_attended, value_h.T, preferred_element_type=jnp.float32)
            grad_scores = jnp.where(
                allowed, grad_weights / length_b * silu_slope(scores), 0.0
            ).astype(jnp.bfloat16)
            grad_query_b = jnp.dot(grad_scores, key_h, preferred_element_type=jnp.float32) * scale
            grad_key_sum = (
                grad_key_sum
                + jnp.dot(grad_scores.T, query_h, preferred_element_type=jnp.float32) * scale
            )
            grad_value_sum = grad_value_sum + jnp.dot(
                weights.T, grad_attended, preferred_element_type=jnp.float32
            )
            return ((grad_key_sum, grad_value_sum), (mixer_b, grad_gate_b, grad_query_b))

        start_sums = (jnp.zeros((rows, DH), jnp.float32), jnp.zeros((rows, DH), jnp.float32))
        (grad_key, grad_value), stacked = lax.scan(block_step, start_sums, jnp.arange(blocks))
        mixer_h = stacked[0].reshape(rows, DH)
        grad_gate = stacked[1].reshape(rows, DH)
        grad_query = stacked[2].reshape(rows, DH)
        mixer_h, grad_gate, grad_query, grad_key, grad_value = (
            mixer_h,
            grad_gate,
            grad_query,
            grad_key,
            grad_value,
        )
        before_act = projected[:, head]
        mixer_parts.append(mixer_h)
        grad_parts.append(
            jnp.stack(
                [
                    grad_gate * silu_slope(before_act[:, 0]),
                    grad_value,
                    grad_query * silu_slope(before_act[:, 2]),
                    grad_key * silu_slope(before_act[:, 3]),
                ],
                axis=1,
            )
        )
    mixer = jnp.concatenate(mixer_parts, axis=1)
    grad_proj = (
        jnp.stack(grad_parts, axis=1).astype(jnp.bfloat16).reshape(rows, heads_here * 4 * DH)
    )
    own_wide = own_tokens.astype(jnp.float32)
    mix_partial = jnp.dot(mixer, w_out, preferred_element_type=jnp.float32)
    out_term = jnp.dot(full_cotangent.T, mixer, preferred_element_type=jnp.float32)
    proj_term = jnp.dot(normed.T, grad_proj, preferred_element_type=jnp.float32).reshape(
        normed.shape[1], heads_here, 4 * DH
    )
    heads_count = lax.axis_size("heads")
    normed_partial = jnp.dot(grad_proj, proj_matrix.T, preferred_element_type=jnp.float32)
    partial_totals = jnp.sum(normed_partial * (tokens_wide * gain[None, :]), axis=1)
    extra = -(-rows // width)
    partial_totals = jnp.pad(partial_totals, (0, extra * width - rows)).reshape(1, extra, width)
    reduced = lax.psum_scatter(
        jnp.concatenate(
            [
                normed_partial.reshape(rows, heads_count, width).transpose(1, 0, 2),
                jnp.broadcast_to(partial_totals, (heads_count, extra, width)),
                mix_partial.reshape(rows, heads_count, width).transpose(1, 0, 2),
            ],
            axis=1,
        ).astype(jnp.bfloat16),
        "heads",
        scatter_dimension=0,
        tiled=True,
    ).astype(jnp.float32)
    grad_normed = reduced[0, :rows]
    row_totals = reduced[0, rows : rows + extra].reshape(-1)[:rows]
    mixed_own = (own_wide + reduced[0, rows + extra :]).astype(jnp.bfloat16)
    gain_share = lax.dynamic_slice_in_dim(gain, lax.axis_index("heads") * width, width)
    grad_scaled = grad_normed * gain_share[None, :]
    input_own = (
        own_cotangent.astype(jnp.float32)
        + inv_rms * grad_scaled
        - own_wide * (inv_rms * inv_rms * inv_rms) * (row_totals / D)[:, None]
    ).astype(jnp.bfloat16)
    norm_factor = 1.0 / math.sqrt(groups * rows)
    proj_cols = heads_here * 4 * DH
    weight_terms = jnp.concatenate(
        [proj_term.reshape(normed.shape[1], proj_cols), out_term], axis=1
    ).reshape(groups, normed.shape[1] // groups, proj_cols + out_term.shape[1])
    weight_sums = jnp.sum(
        lax.all_to_all(
            weight_terms.astype(jnp.bfloat16), "users", split_axis=0, concat_axis=0, tiled=True
        ).astype(jnp.float32),
        axis=0,
    )
    proj_sum = weight_sums[:, :proj_cols].reshape(-1, heads_here, 4 * DH)
    out_sum = weight_sums[:, proj_cols:]
    grad_tiles = select_tiles(input_own.reshape(per_owner, TILE, width), back_index, back_valid)
    mixed_tiles = select_tiles(mixed_own.reshape(per_owner, TILE, width), back_index, back_valid)
    home = lax.all_to_all(
        jnp.stack([mixed_tiles, grad_tiles], axis=1),
        "users",
        split_axis=0,
        concat_axis=0,
        tiled=True,
    )
    mixed = jnp.take(home[:, 0], home_index, axis=0).reshape(rows, width)
    input_grad = jnp.take(home[:, 1], home_index, axis=0).reshape(rows, width)
    return (mixed, input_grad, proj_sum * norm_factor, out_sum * norm_factor)


def solution(mesh):
    placed = (
        P("users", "heads"),
        P("users", "heads"),
        P(),
        P(None, "heads", None),
        P("heads", None),
        P(),
        P("users"),
        P("users"),
    )
    return jax.shard_map(
        per_device,
        mesh=mesh,
        in_specs=placed,
        out_specs=(
            P("users", "heads"),
            P("users", "heads"),
            P("users", "heads", None),
            P("users", "heads"),
        ),
        check_vma=False,
    )
```

```python
import math

import jax
import jax.numpy as jnp
from jax import lax
from jax.sharding import PartitionSpec as P

D = 1024
DH = 64
TILE = 128
CAP = 1


norm_eps = 1e-05


def silu_slope(value):
    sigma = jax.nn.sigmoid(value)
    return sigma * (1.0 + value * (1.0 - sigma))


def route_tables(arrival_slot, owner_index, groups, per_owner):
    placed = arrival_slot.reshape(groups, per_owner)
    owners = placed // per_owner
    tile_ids = jnp.arange(per_owner, dtype=jnp.int32)
    same_owner = owners[:, :, None] == owners[:, None, :]
    earlier = tile_ids[None, :] < tile_ids[:, None]
    ranks = jnp.sum((same_owner & earlier[None, :, :]).astype(jnp.int32), axis=2)
    my_owners = lax.dynamic_index_in_dim(owners, owner_index, 0, keepdims=False)
    my_ranks = lax.dynamic_index_in_dim(ranks, owner_index, 0, keepdims=False)
    buffer_ids = jnp.arange(groups * CAP, dtype=jnp.int32)
    peers = buffer_ids // CAP
    turns = buffer_ids % CAP
    chosen = (my_owners[None, :] == peers[:, None]) & (my_ranks[None, :] == turns[:, None])
    send_index = jnp.sum(chosen.astype(jnp.int32) * tile_ids[None, :], axis=1)
    send_valid = jnp.any(chosen, axis=1)
    codes = (jnp.arange(groups, dtype=jnp.int32)[:, None] * CAP + ranks).reshape(-1)
    wanted = owner_index * per_owner + tile_ids
    matches = placed.reshape(-1)[None, :] == wanted[:, None]
    receive_index = jnp.sum(matches.astype(jnp.int32) * codes[None, :], axis=1)
    owner_lines = jnp.repeat(owners, CAP, axis=0)
    rank_lines = jnp.repeat(ranks, CAP, axis=0)
    place_lines = jnp.repeat(placed, CAP, axis=0)
    returning = (owner_lines == owner_index) & (rank_lines == turns[:, None])
    back_index = jnp.sum(
        returning.astype(jnp.int32) * (place_lines - owner_index * per_owner), axis=1
    )
    back_valid = jnp.any(returning, axis=1)
    home_index = my_owners * CAP + my_ranks
    return (send_index, send_valid, receive_index, back_index, back_valid, home_index)


def select_tiles(tiles, index, keep):
    taken = jnp.take(tiles, index, axis=0)
    return jnp.where(keep[:, None, None], taken, jnp.zeros_like(taken))


def per_device(tokens, cotangent, gain, w_proj, w_out, arrival_slot, user_start, user_length):
    groups = lax.axis_size("users")
    owner_index = lax.axis_index("users")
    rows, width = tokens.shape
    per_owner = rows // TILE
    heads_here = w_proj.shape[1]
    scale = DH ** (-0.5)
    send_index, send_valid, receive_index, back_index, back_valid, home_index = route_tables(
        arrival_slot, owner_index, groups, per_owner
    )
    outgoing_tokens = select_tiles(tokens.reshape(per_owner, TILE, width), send_index, send_valid)
    outgoing_grads = select_tiles(cotangent.reshape(per_owner, TILE, width), send_index, send_valid)
    arrived = lax.all_to_all(
        jnp.stack([outgoing_tokens, outgoing_grads], axis=1),
        "users",
        split_axis=0,
        concat_axis=0,
        tiled=True,
    )
    own_both = jnp.take(arrived, receive_index, axis=0)
    own_tokens = own_both[:, 0].reshape(rows, width)
    own_cotangent = own_both[:, 1].reshape(rows, width)
    full_both = lax.all_gather(own_both, "heads", axis=3, tiled=True)
    full_tokens = full_both[:, 0].reshape(rows, -1)
    full_cotangent = full_both[:, 1].reshape(rows, -1)
    tokens_wide = full_tokens.astype(jnp.float32)
    inv_rms = lax.rsqrt(jnp.mean(tokens_wide * tokens_wide, axis=1, keepdims=True) + norm_eps)
    normed = (tokens_wide * inv_rms * gain[None, :]).astype(jnp.bfloat16)
    proj_matrix = w_proj.reshape(w_proj.shape[0], heads_here * 4 * DH)
    projected = jnp.dot(normed, proj_matrix, preferred_element_type=jnp.float32).reshape(
        rows, heads_here, 4, DH
    )
    gate_rows = jax.nn.silu(projected[:, :, 0]).astype(jnp.bfloat16)
    value_rows = projected[:, :, 1].astype(jnp.bfloat16)
    query_rows = jax.nn.silu(projected[:, :, 2]).astype(jnp.bfloat16)
    key_rows = jax.nn.silu(projected[:, :, 3]).astype(jnp.bfloat16)
    grad_mix = (
        jnp.dot(full_cotangent, w_out.T, preferred_element_type=jnp.float32)
        .astype(jnp.bfloat16)
        .reshape(rows, heads_here, DH)
    )
    row_ids = jnp.arange(rows, dtype=jnp.int32)
    first = jnp.repeat(user_start, TILE)
    length = jnp.repeat(user_length, TILE)
    position = (row_ids // TILE - first) * TILE + row_ids % TILE
    is_live = position < length
    length_wide = length.astype(jnp.float32)
    blocks = 1
    mixer_parts = []
    grad_parts = []
    for head in range(heads_here):
        query_h = query_rows[:, head]
        key_h = key_rows[:, head]
        value_h = value_rows[:, head]
        gate_h = gate_rows[:, head]
        grad_mix_h = grad_mix[:, head]

        def block_step(carry, block):
            grad_key_sum, grad_value_sum = carry
            allowed = (
                (first[:, None] == first[None, :])
                & (position[None, :] <= position[:, None])
                & is_live[:, None]
                & is_live[None, :]
            )
            length_b = length_wide[:, None]
            scores = jnp.dot(query_h, key_h.T, preferred_element_type=jnp.float32) * scale
            weights = jnp.where(allowed, jax.nn.silu(scores) / length_b, 0.0).astype(jnp.bfloat16)
            attended = jnp.dot(weights, value_h, preferred_element_type=jnp.float32)
            inv_attn = lax.rsqrt(jnp.mean(attended * attended, axis=1, keepdims=True) + norm_eps)
            attn_normed = attended * inv_attn
            gate_wide = gate_h.astype(jnp.float32)
            grad_mix_wide = grad_mix_h.astype(jnp.float32)
            mixer_b = (attn_normed * gate_wide).astype(jnp.bfloat16)
            grad_gate_b = grad_mix_wide * attn_normed
            grad_attn_normed = grad_mix_wide * gate_wide
            grad_attended = (
                inv_attn
                * (
                    grad_attn_normed
                    - attn_normed * jnp.mean(grad_attn_normed * attn_normed, axis=1, keepdims=True)
                )
            ).astype(jnp.bfloat16)
            grad_weights = jnp.dot(grad_attended, value_h.T, preferred_element_type=jnp.float32)
            grad_scores = jnp.where(
                allowed, grad_weights / length_b * silu_slope(scores), 0.0
            ).astype(jnp.bfloat16)
            grad_query_b = jnp.dot(grad_scores, key_h, preferred_element_type=jnp.float32) * scale
            grad_key_sum = (
                grad_key_sum
                + jnp.dot(grad_scores.T, query_h, preferred_element_type=jnp.float32) * scale
            )
            grad_value_sum = grad_value_sum + jnp.dot(
                weights.T, grad_attended, preferred_element_type=jnp.float32
            )
            return ((grad_key_sum, grad_value_sum), (mixer_b, grad_gate_b, grad_query_b))

        start_sums = (jnp.zeros((rows, DH), jnp.float32), jnp.zeros((rows, DH), jnp.float32))
        (grad_key, grad_value), stacked = lax.scan(block_step, start_sums, jnp.arange(blocks))
        mixer_h = stacked[0].reshape(rows, DH)
        grad_gate = stacked[1].reshape(rows, DH)
        grad_query = stacked[2].reshape(rows, DH)
        mixer_h, grad_gate, grad_query, grad_key, grad_value = (
            mixer_h,
            grad_gate,
            grad_query,
            grad_key,
            grad_value,
        )
        before_act = projected[:, head]
        mixer_parts.append(mixer_h)
        grad_parts.append(
            jnp.stack(
                [
                    grad_gate * silu_slope(before_act[:, 0]),
                    grad_value,
                    grad_query * silu_slope(before_act[:, 2]),
                    grad_key * silu_slope(before_act[:, 3]),
                ],
                axis=1,
            )
        )
    mixer = jnp.concatenate(mixer_parts, axis=1)
    grad_proj = (
        jnp.stack(grad_parts, axis=1).astype(jnp.bfloat16).reshape(rows, heads_here * 4 * DH)
    )
    own_wide = own_tokens.astype(jnp.float32)
    mix_partial = jnp.dot(mixer, w_out, preferred_element_type=jnp.float32)
    out_term = jnp.dot(full_cotangent.T, mixer, preferred_element_type=jnp.float32)
    proj_term = jnp.dot(normed.T, grad_proj, preferred_element_type=jnp.float32).reshape(
        normed.shape[1], heads_here, 4 * DH
    )
    heads_count = lax.axis_size("heads")
    normed_partial = jnp.dot(grad_proj, proj_matrix.T, preferred_element_type=jnp.float32)
    partial_totals = jnp.sum(
        grad_proj.astype(jnp.float32) * projected.reshape(rows, -1), axis=1
    ) / inv_rms[:, 0]
    extra = -(-rows // width)
    partial_totals = jnp.pad(partial_totals, (0, extra * width - rows)).reshape(1, extra, width)
    reduced = lax.psum_scatter(
        jnp.concatenate(
            [
                normed_partial.reshape(rows, heads_count, width).transpose(1, 0, 2),
                jnp.broadcast_to(partial_totals, (heads_count, extra, width)),
                mix_partial.reshape(rows, heads_count, width).transpose(1, 0, 2),
            ],
            axis=1,
        ).astype(jnp.bfloat16),
        "heads",
        scatter_dimension=0,
        tiled=True,
    ).astype(jnp.float32)
    grad_normed = reduced[0, :rows]
    row_totals = reduced[0, rows : rows + extra].reshape(-1)[:rows]
    mixed_own = (own_wide + reduced[0, rows + extra :]).astype(jnp.bfloat16)
    gain_share = lax.dynamic_slice_in_dim(gain, lax.axis_index("heads") * width, width)
    grad_scaled = grad_normed * gain_share[None, :]
    input_own = (
        own_cotangent.astype(jnp.float32)
        + inv_rms * grad_scaled
        - own_wide * (inv_rms * inv_rms * inv_rms) * (row_totals / D)[:, None]
    ).astype(jnp.bfloat16)
    norm_factor = 1.0 / math.sqrt(groups * rows)
    proj_cols = heads_here * 4 * DH
    weight_terms = jnp.concatenate(
        [proj_term.reshape(normed.shape[1], proj_cols), out_term], axis=1
    ).reshape(groups, normed.shape[1] // groups, proj_cols + out_term.shape[1])
    weight_sums = jnp.sum(
        lax.all_to_all(
            weight_terms.astype(jnp.bfloat16), "users", split_axis=0, concat_axis=0, tiled=True
        ).astype(jnp.float32),
        axis=0,
    )
    proj_sum = weight_sums[:, :proj_cols].reshape(-1, heads_here, 4 * DH)
    out_sum = weight_sums[:, proj_cols:]
    grad_tiles = select_tiles(input_own.reshape(per_owner, TILE, width), back_index, back_valid)
    mixed_tiles = select_tiles(mixed_own.reshape(per_owner, TILE, width), back_index, back_valid)
    home = lax.all_to_all(
        jnp.stack([mixed_tiles, grad_tiles], axis=1),
        "users",
        split_axis=0,
        concat_axis=0,
        tiled=True,
    )
    mixed = jnp.take(home[:, 0], home_index, axis=0).reshape(rows, width)
    input_grad = jnp.take(home[:, 1], home_index, axis=0).reshape(rows, width)
    return (mixed, input_grad, proj_sum * norm_factor, out_sum * norm_factor)


def solution(mesh):
    placed = (
        P("users", "heads"),
        P("users", "heads"),
        P(),
        P(None, "heads", None),
        P("heads", None),
        P(),
        P("users"),
        P("users"),
    )
    return jax.shard_map(
        per_device,
        mesh=mesh,
        in_specs=placed,
        out_specs=(
            P("users", "heads"),
            P("users", "heads"),
            P("users", "heads", None),
            P("users", "heads"),
        ),
        check_vma=False,
    )
```

```python
import math

import jax
import jax.numpy as jnp
from jax import lax
from jax.sharding import PartitionSpec as P

D = 1024
DH = 64
TILE = 128
CAP = 1


norm_eps = 1e-05


def silu_slope(value):
    sigma = jax.nn.sigmoid(value)
    return sigma * (1.0 + value * (1.0 - sigma))


def route_tables(arrival_slot, owner_index, groups, per_owner):
    placed = arrival_slot.reshape(groups, per_owner)
    owners = placed // per_owner
    tile_ids = jnp.arange(per_owner, dtype=jnp.int32)
    same_owner = owners[:, :, None] == owners[:, None, :]
    earlier = tile_ids[None, :] < tile_ids[:, None]
    ranks = jnp.sum((same_owner & earlier[None, :, :]).astype(jnp.int32), axis=2)
    my_owners = lax.dynamic_index_in_dim(owners, owner_index, 0, keepdims=False)
    my_ranks = lax.dynamic_index_in_dim(ranks, owner_index, 0, keepdims=False)
    buffer_ids = jnp.arange(groups * CAP, dtype=jnp.int32)
    peers = buffer_ids // CAP
    turns = buffer_ids % CAP
    chosen = (my_owners[None, :] == peers[:, None]) & (my_ranks[None, :] == turns[:, None])
    send_index = jnp.sum(chosen.astype(jnp.int32) * tile_ids[None, :], axis=1)
    send_valid = jnp.any(chosen, axis=1)
    codes = (jnp.arange(groups, dtype=jnp.int32)[:, None] * CAP + ranks).reshape(-1)
    wanted = owner_index * per_owner + tile_ids
    matches = placed.reshape(-1)[None, :] == wanted[:, None]
    receive_index = jnp.sum(matches.astype(jnp.int32) * codes[None, :], axis=1)
    owner_lines = jnp.repeat(owners, CAP, axis=0)
    rank_lines = jnp.repeat(ranks, CAP, axis=0)
    place_lines = jnp.repeat(placed, CAP, axis=0)
    returning = (owner_lines == owner_index) & (rank_lines == turns[:, None])
    back_index = jnp.sum(
        returning.astype(jnp.int32) * (place_lines - owner_index * per_owner), axis=1
    )
    back_valid = jnp.any(returning, axis=1)
    home_index = my_owners * CAP + my_ranks
    return (send_index, send_valid, receive_index, back_index, back_valid, home_index)


def select_tiles(tiles, index, keep):
    taken = jnp.take(tiles, index, axis=0)
    return jnp.where(keep[:, None, None], taken, jnp.zeros_like(taken))


def per_device(tokens, cotangent, gain, w_proj, w_out, arrival_slot, user_start, user_length):
    groups = lax.axis_size("users")
    owner_index = lax.axis_index("users")
    rows, width = tokens.shape
    per_owner = rows // TILE
    heads_here = w_proj.shape[1]
    scale = DH ** (-0.5)
    send_index, send_valid, receive_index, back_index, back_valid, home_index = route_tables(
        arrival_slot, owner_index, groups, per_owner
    )
    outgoing_tokens = select_tiles(tokens.reshape(per_owner, TILE, width), send_index, send_valid)
    outgoing_grads = select_tiles(cotangent.reshape(per_owner, TILE, width), send_index, send_valid)
    arrived = lax.all_to_all(
        jnp.stack([outgoing_tokens, outgoing_grads], axis=1),
        "users",
        split_axis=0,
        concat_axis=0,
        tiled=True,
    )
    own_both = jnp.take(arrived, receive_index, axis=0)
    own_tokens = own_both[:, 0].reshape(rows, width)
    own_cotangent = own_both[:, 1].reshape(rows, width)
    full_both = lax.all_gather(own_both, "heads", axis=3, tiled=True)
    full_tokens = full_both[:, 0].reshape(rows, -1)
    full_cotangent = full_both[:, 1].reshape(rows, -1)
    tokens_wide = full_tokens.astype(jnp.float32)
    inv_rms = lax.rsqrt(jnp.mean(tokens_wide * tokens_wide, axis=1, keepdims=True) + norm_eps)
    normed = (tokens_wide * inv_rms * gain[None, :]).astype(jnp.bfloat16)
    proj_matrix = w_proj.reshape(w_proj.shape[0], heads_here * 4 * DH)
    projected = jnp.dot(normed, proj_matrix, preferred_element_type=jnp.float32).reshape(
        rows, heads_here, 4, DH
    )
    gate_rows = jax.nn.silu(projected[:, :, 0]).astype(jnp.bfloat16)
    value_rows = projected[:, :, 1].astype(jnp.bfloat16)
    query_rows = jax.nn.silu(projected[:, :, 2]).astype(jnp.bfloat16)
    key_rows = jax.nn.silu(projected[:, :, 3]).astype(jnp.bfloat16)
    grad_mix = (
        jnp.dot(full_cotangent, w_out.T, preferred_element_type=jnp.float32)
        .astype(jnp.bfloat16)
        .reshape(rows, heads_here, DH)
    )
    row_ids = jnp.arange(rows, dtype=jnp.int32)
    first = jnp.repeat(user_start, TILE)
    length = jnp.repeat(user_length, TILE)
    position = (row_ids // TILE - first) * TILE + row_ids % TILE
    is_live = position < length
    length_wide = length.astype(jnp.float32)
    blocks = 1
    mixer_parts = []
    grad_parts = []
    for head in range(heads_here):
        query_h = query_rows[:, head]
        key_h = key_rows[:, head]
        value_h = value_rows[:, head]
        gate_h = gate_rows[:, head]
        grad_mix_h = grad_mix[:, head]

        def block_step(carry, block):
            grad_key_sum, grad_value_sum = carry
            allowed = (
                (first[:, None] == first[None, :])
                & (position[None, :] <= position[:, None])
                & is_live[:, None]
                & is_live[None, :]
            )
            length_b = length_wide[:, None]
            scores = jnp.dot(query_h, key_h.T, preferred_element_type=jnp.float32) * scale
            weights = jnp.where(allowed, jax.nn.silu(scores) / length_b, 0.0).astype(jnp.bfloat16)
            attended = jnp.dot(weights, value_h, preferred_element_type=jnp.float32)
            inv_attn = lax.rsqrt(jnp.mean(attended * attended, axis=1, keepdims=True) + norm_eps)
            attn_normed = attended * inv_attn
            gate_wide = gate_h.astype(jnp.float32)
            grad_mix_wide = grad_mix_h.astype(jnp.float32)
            mixer_b = (attn_normed * gate_wide).astype(jnp.bfloat16)
            grad_gate_b = grad_mix_wide * attn_normed
            grad_attn_normed = grad_mix_wide * gate_wide
            grad_attended = (
                inv_attn
                * (
                    grad_attn_normed
                    - attn_normed * jnp.mean(grad_attn_normed * attn_normed, axis=1, keepdims=True)
                )
            ).astype(jnp.bfloat16)
            grad_weights = jnp.dot(grad_attended, value_h.T, preferred_element_type=jnp.float32)
            grad_scores = jnp.where(
                allowed, grad_weights / length_b * silu_slope(scores), 0.0
            ).astype(jnp.bfloat16)
            grad_query_b = jnp.dot(grad_scores, key_h, preferred_element_type=jnp.float32) * scale
            grad_key_sum = (
                grad_key_sum
                + jnp.dot(grad_scores.T, query_h, preferred_element_type=jnp.float32) * scale
            )
            grad_value_sum = grad_value_sum + jnp.dot(
                weights.T, grad_attended, preferred_element_type=jnp.float32
            )
            return ((grad_key_sum, grad_value_sum), (mixer_b, grad_gate_b, grad_query_b))

        start_sums = (jnp.zeros((rows, DH), jnp.float32), jnp.zeros((rows, DH), jnp.float32))
        (grad_key, grad_value), stacked = lax.scan(block_step, start_sums, jnp.arange(blocks))
        mixer_h = stacked[0].reshape(rows, DH)
        grad_gate = stacked[1].reshape(rows, DH)
        grad_query = stacked[2].reshape(rows, DH)
        mixer_h, grad_gate, grad_query, grad_key, grad_value = (
            mixer_h,
            grad_gate,
            grad_query,
            grad_key,
            grad_value,
        )
        before_act = projected[:, head]
        mixer_parts.append(mixer_h)
        grad_parts.append(
            jnp.stack(
                [
                    grad_gate * silu_slope(before_act[:, 0]),
                    grad_value,
                    grad_query * silu_slope(before_act[:, 2]),
                    grad_key * silu_slope(before_act[:, 3]),
                ],
                axis=1,
            )
        )
    mixer = jnp.concatenate(mixer_parts, axis=1)
    grad_proj = (
        jnp.stack(grad_parts, axis=1).astype(jnp.bfloat16).reshape(rows, heads_here * 4 * DH)
    )
    own_wide = own_tokens.astype(jnp.float32)
    heads_count = lax.axis_size("heads")
    mix_partial = jnp.einsum(
        "rk,khf->hrf",
        mixer,
        w_out.reshape(w_out.shape[0], heads_count, width),
        preferred_element_type=jnp.float32,
    )
    out_term = jnp.dot(full_cotangent.T, mixer, preferred_element_type=jnp.float32)
    proj_term = jnp.dot(normed.T, grad_proj, preferred_element_type=jnp.float32).reshape(
        normed.shape[1], heads_here, 4 * DH
    )
    normed_partial = jnp.einsum(
        "rk,hfk->hrf",
        grad_proj,
        proj_matrix.reshape(heads_count, width, proj_matrix.shape[1]),
        preferred_element_type=jnp.float32,
    )
    partial_totals = jnp.sum(
        grad_proj.astype(jnp.float32) * projected.reshape(rows, -1), axis=1
    ) / inv_rms[:, 0]
    extra = -(-rows // width)
    partial_totals = jnp.pad(partial_totals, (0, extra * width - rows)).reshape(1, extra, width)
    reduced = lax.psum_scatter(
        jnp.concatenate(
            [
                normed_partial,
                jnp.broadcast_to(partial_totals, (heads_count, extra, width)),
                mix_partial,
            ],
            axis=1,
        ).astype(jnp.bfloat16),
        "heads",
        scatter_dimension=0,
        tiled=True,
    ).astype(jnp.float32)
    grad_normed = reduced[0, :rows]
    row_totals = reduced[0, rows : rows + extra].reshape(-1)[:rows]
    mixed_own = (own_wide + reduced[0, rows + extra :]).astype(jnp.bfloat16)
    gain_share = lax.dynamic_slice_in_dim(gain, lax.axis_index("heads") * width, width)
    grad_scaled = grad_normed * gain_share[None, :]
    input_own = (
        own_cotangent.astype(jnp.float32)
        + inv_rms * grad_scaled
        - own_wide * (inv_rms * inv_rms * inv_rms) * (row_totals / D)[:, None]
    ).astype(jnp.bfloat16)
    norm_factor = 1.0 / math.sqrt(groups * rows)
    proj_cols = heads_here * 4 * DH
    weight_terms = jnp.concatenate(
        [proj_term.reshape(normed.shape[1], proj_cols), out_term], axis=1
    ).reshape(groups, normed.shape[1] // groups, proj_cols + out_term.shape[1])
    weight_sums = jnp.sum(
        lax.all_to_all(
            weight_terms.astype(jnp.bfloat16), "users", split_axis=0, concat_axis=0, tiled=True
        ).astype(jnp.float32),
        axis=0,
    )
    proj_sum = weight_sums[:, :proj_cols].reshape(-1, heads_here, 4 * DH)
    out_sum = weight_sums[:, proj_cols:]
    grad_tiles = select_tiles(input_own.reshape(per_owner, TILE, width), back_index, back_valid)
    mixed_tiles = select_tiles(mixed_own.reshape(per_owner, TILE, width), back_index, back_valid)
    home = lax.all_to_all(
        jnp.stack([mixed_tiles, grad_tiles], axis=1),
        "users",
        split_axis=0,
        concat_axis=0,
        tiled=True,
    )
    mixed = jnp.take(home[:, 0], home_index, axis=0).reshape(rows, width)
    input_grad = jnp.take(home[:, 1], home_index, axis=0).reshape(rows, width)
    return (mixed, input_grad, proj_sum * norm_factor, out_sum * norm_factor)


def solution(mesh):
    placed = (
        P("users", "heads"),
        P("users", "heads"),
        P(),
        P(None, "heads", None),
        P("heads", None),
        P(),
        P("users"),
        P("users"),
    )
    return jax.shard_map(
        per_device,
        mesh=mesh,
        in_specs=placed,
        out_specs=(
            P("users", "heads"),
            P("users", "heads"),
            P("users", "heads", None),
            P("users", "heads"),
        ),
        check_vma=False,
    )
```

```python
import math

import jax
import jax.numpy as jnp
from jax import lax
from jax.sharding import PartitionSpec as P

D = 1024
DH = 64
TILE = 128
CAP = 1


norm_eps = 1e-05


def silu_slope(value):
    sigma = jax.nn.sigmoid(value)
    return sigma * (1.0 + value * (1.0 - sigma))


def route_tables(arrival_slot, owner_index, groups, per_owner):
    placed = arrival_slot.reshape(groups, per_owner)
    owners = placed // per_owner
    tile_ids = jnp.arange(per_owner, dtype=jnp.int32)
    same_owner = owners[:, :, None] == owners[:, None, :]
    earlier = tile_ids[None, :] < tile_ids[:, None]
    ranks = jnp.sum((same_owner & earlier[None, :, :]).astype(jnp.int32), axis=2)
    my_owners = lax.dynamic_index_in_dim(owners, owner_index, 0, keepdims=False)
    my_ranks = lax.dynamic_index_in_dim(ranks, owner_index, 0, keepdims=False)
    buffer_ids = jnp.arange(groups * CAP, dtype=jnp.int32)
    peers = buffer_ids // CAP
    turns = buffer_ids % CAP
    chosen = (my_owners[None, :] == peers[:, None]) & (my_ranks[None, :] == turns[:, None])
    send_index = jnp.sum(chosen.astype(jnp.int32) * tile_ids[None, :], axis=1)
    send_valid = jnp.any(chosen, axis=1)
    codes = (jnp.arange(groups, dtype=jnp.int32)[:, None] * CAP + ranks).reshape(-1)
    wanted = owner_index * per_owner + tile_ids
    matches = placed.reshape(-1)[None, :] == wanted[:, None]
    receive_index = jnp.sum(matches.astype(jnp.int32) * codes[None, :], axis=1)
    owner_lines = jnp.repeat(owners, CAP, axis=0)
    rank_lines = jnp.repeat(ranks, CAP, axis=0)
    place_lines = jnp.repeat(placed, CAP, axis=0)
    returning = (owner_lines == owner_index) & (rank_lines == turns[:, None])
    back_index = jnp.sum(
        returning.astype(jnp.int32) * (place_lines - owner_index * per_owner), axis=1
    )
    back_valid = jnp.any(returning, axis=1)
    home_index = my_owners * CAP + my_ranks
    return (send_index, send_valid, receive_index, back_index, back_valid, home_index)


def select_tiles(tiles, index, keep):
    del keep
    return jnp.take(tiles, index, axis=0)


def per_device(tokens, cotangent, gain, w_proj, w_out, arrival_slot, user_start, user_length):
    groups = lax.axis_size("users")
    owner_index = lax.axis_index("users")
    rows, width = tokens.shape
    per_owner = rows // TILE
    heads_here = w_proj.shape[1]
    scale = DH ** (-0.5)
    send_index, send_valid, receive_index, back_index, back_valid, home_index = route_tables(
        arrival_slot, owner_index, groups, per_owner
    )
    outgoing_tokens = select_tiles(tokens.reshape(per_owner, TILE, width), send_index, send_valid)
    outgoing_grads = select_tiles(cotangent.reshape(per_owner, TILE, width), send_index, send_valid)
    arrived = lax.all_to_all(
        jnp.stack([outgoing_tokens, outgoing_grads], axis=1),
        "users",
        split_axis=0,
        concat_axis=0,
        tiled=True,
    )
    own_both = jnp.take(arrived, receive_index, axis=0)
    own_tokens = own_both[:, 0].reshape(rows, width)
    own_cotangent = own_both[:, 1].reshape(rows, width)
    full_both = lax.all_gather(own_both, "heads", axis=3, tiled=True)
    full_tokens = full_both[:, 0].reshape(rows, -1)
    full_cotangent = full_both[:, 1].reshape(rows, -1)
    tokens_wide = full_tokens.astype(jnp.float32)
    inv_rms = lax.rsqrt(jnp.mean(tokens_wide * tokens_wide, axis=1, keepdims=True) + norm_eps)
    normed = (tokens_wide * inv_rms * gain[None, :]).astype(jnp.bfloat16)
    proj_matrix = w_proj.reshape(w_proj.shape[0], heads_here * 4 * DH)
    projected = jnp.dot(normed, proj_matrix, preferred_element_type=jnp.float32).reshape(
        rows, heads_here, 4, DH
    )
    gate_rows = jax.nn.silu(projected[:, :, 0]).astype(jnp.bfloat16)
    value_rows = projected[:, :, 1].astype(jnp.bfloat16)
    query_rows = jax.nn.silu(projected[:, :, 2]).astype(jnp.bfloat16)
    key_rows = jax.nn.silu(projected[:, :, 3]).astype(jnp.bfloat16)
    grad_mix = (
        jnp.dot(full_cotangent, w_out.T, preferred_element_type=jnp.float32)
        .astype(jnp.bfloat16)
        .reshape(rows, heads_here, DH)
    )
    row_ids = jnp.arange(rows, dtype=jnp.int32)
    first = jnp.repeat(user_start, TILE)
    length = jnp.repeat(user_length, TILE)
    position = (row_ids // TILE - first) * TILE + row_ids % TILE
    is_live = position < length
    length_wide = length.astype(jnp.float32)
    blocks = 1
    mixer_parts = []
    grad_parts = []
    for head in range(heads_here):
        query_h = query_rows[:, head]
        key_h = key_rows[:, head]
        value_h = value_rows[:, head]
        gate_h = gate_rows[:, head]
        grad_mix_h = grad_mix[:, head]

        def block_step(carry, block):
            grad_key_sum, grad_value_sum = carry
            allowed = (
                (first[:, None] == first[None, :])
                & (position[None, :] <= position[:, None])
                & is_live[:, None]
                & is_live[None, :]
            )
            length_b = length_wide[:, None]
            scores = jnp.dot(query_h, key_h.T, preferred_element_type=jnp.float32) * scale
            weights = jnp.where(allowed, jax.nn.silu(scores) / length_b, 0.0).astype(jnp.bfloat16)
            attended = jnp.dot(weights, value_h, preferred_element_type=jnp.float32)
            inv_attn = lax.rsqrt(jnp.mean(attended * attended, axis=1, keepdims=True) + norm_eps)
            attn_normed = attended * inv_attn
            gate_wide = gate_h.astype(jnp.float32)
            grad_mix_wide = grad_mix_h.astype(jnp.float32)
            mixer_b = (attn_normed * gate_wide).astype(jnp.bfloat16)
            grad_gate_b = grad_mix_wide * attn_normed
            grad_attn_normed = grad_mix_wide * gate_wide
            grad_attended = (
                inv_attn
                * (
                    grad_attn_normed
                    - attn_normed * jnp.mean(grad_attn_normed * attn_normed, axis=1, keepdims=True)
                )
            ).astype(jnp.bfloat16)
            grad_weights = jnp.dot(grad_attended, value_h.T, preferred_element_type=jnp.float32)
            grad_scores = jnp.where(
                allowed, grad_weights / length_b * silu_slope(scores), 0.0
            ).astype(jnp.bfloat16)
            grad_query_b = jnp.dot(grad_scores, key_h, preferred_element_type=jnp.float32) * scale
            grad_key_sum = (
                grad_key_sum
                + jnp.dot(grad_scores.T, query_h, preferred_element_type=jnp.float32) * scale
            )
            grad_value_sum = grad_value_sum + jnp.dot(
                weights.T, grad_attended, preferred_element_type=jnp.float32
            )
            return ((grad_key_sum, grad_value_sum), (mixer_b, grad_gate_b, grad_query_b))

        start_sums = (jnp.zeros((rows, DH), jnp.float32), jnp.zeros((rows, DH), jnp.float32))
        (grad_key, grad_value), stacked = lax.scan(block_step, start_sums, jnp.arange(blocks))
        mixer_h = stacked[0].reshape(rows, DH)
        grad_gate = stacked[1].reshape(rows, DH)
        grad_query = stacked[2].reshape(rows, DH)
        mixer_h, grad_gate, grad_query, grad_key, grad_value = (
            mixer_h,
            grad_gate,
            grad_query,
            grad_key,
            grad_value,
        )
        before_act = projected[:, head]
        mixer_parts.append(mixer_h)
        grad_parts.append(
            jnp.stack(
                [
                    grad_gate * silu_slope(before_act[:, 0]),
                    grad_value,
                    grad_query * silu_slope(before_act[:, 2]),
                    grad_key * silu_slope(before_act[:, 3]),
                ],
                axis=1,
            )
        )
    mixer = jnp.concatenate(mixer_parts, axis=1)
    grad_proj = (
        jnp.stack(grad_parts, axis=1).astype(jnp.bfloat16).reshape(rows, heads_here * 4 * DH)
    )
    own_wide = own_tokens.astype(jnp.float32)
    heads_count = lax.axis_size("heads")
    mix_partial = jnp.einsum(
        "rk,khf->hrf",
        mixer,
        w_out.reshape(w_out.shape[0], heads_count, width),
        preferred_element_type=jnp.float32,
    )
    out_term = jnp.dot(full_cotangent.T, mixer, preferred_element_type=jnp.float32)
    proj_term = jnp.dot(normed.T, grad_proj, preferred_element_type=jnp.float32).reshape(
        normed.shape[1], heads_here, 4 * DH
    )
    normed_partial = jnp.einsum(
        "rk,hfk->hrf",
        grad_proj,
        proj_matrix.reshape(heads_count, width, proj_matrix.shape[1]),
        preferred_element_type=jnp.float32,
    )
    partial_totals = jnp.sum(
        grad_proj.astype(jnp.float32) * projected.reshape(rows, -1), axis=1
    ) / inv_rms[:, 0]
    extra = -(-rows // width)
    partial_totals = jnp.pad(partial_totals, (0, extra * width - rows)).reshape(1, extra, width)
    reduced = lax.psum_scatter(
        jnp.concatenate(
            [
                normed_partial,
                jnp.broadcast_to(partial_totals, (heads_count, extra, width)),
                mix_partial,
            ],
            axis=1,
        ).astype(jnp.bfloat16),
        "heads",
        scatter_dimension=0,
        tiled=True,
    ).astype(jnp.float32)
    grad_normed = reduced[0, :rows]
    row_totals = reduced[0, rows : rows + extra].reshape(-1)[:rows]
    mixed_own = (own_wide + reduced[0, rows + extra :]).astype(jnp.bfloat16)
    gain_share = lax.dynamic_slice_in_dim(gain, lax.axis_index("heads") * width, width)
    grad_scaled = grad_normed * gain_share[None, :]
    input_own = (
        own_cotangent.astype(jnp.float32)
        + inv_rms * grad_scaled
        - own_wide * (inv_rms * inv_rms * inv_rms) * (row_totals / D)[:, None]
    ).astype(jnp.bfloat16)
    norm_factor = 1.0 / math.sqrt(groups * rows)
    proj_cols = heads_here * 4 * DH
    weight_terms = jnp.concatenate(
        [proj_term.reshape(normed.shape[1], proj_cols), out_term], axis=1
    ).reshape(groups, normed.shape[1] // groups, proj_cols + out_term.shape[1])
    weight_sums = jnp.sum(
        lax.all_to_all(
            weight_terms.astype(jnp.bfloat16), "users", split_axis=0, concat_axis=0, tiled=True
        ).astype(jnp.float32),
        axis=0,
    )
    proj_sum = weight_sums[:, :proj_cols].reshape(-1, heads_here, 4 * DH)
    out_sum = weight_sums[:, proj_cols:]
    grad_tiles = select_tiles(input_own.reshape(per_owner, TILE, width), back_index, back_valid)
    mixed_tiles = select_tiles(mixed_own.reshape(per_owner, TILE, width), back_index, back_valid)
    home = lax.all_to_all(
        jnp.stack([mixed_tiles, grad_tiles], axis=1),
        "users",
        split_axis=0,
        concat_axis=0,
        tiled=True,
    )
    mixed = jnp.take(home[:, 0], home_index, axis=0).reshape(rows, width)
    input_grad = jnp.take(home[:, 1], home_index, axis=0).reshape(rows, width)
    return (mixed, input_grad, proj_sum * norm_factor, out_sum * norm_factor)


def solution(mesh):
    placed = (
        P("users", "heads"),
        P("users", "heads"),
        P(),
        P(None, "heads", None),
        P("heads", None),
        P(),
        P("users"),
        P("users"),
    )
    return jax.shard_map(
        per_device,
        mesh=mesh,
        in_specs=placed,
        out_specs=(
            P("users", "heads"),
            P("users", "heads"),
            P("users", "heads", None),
            P("users", "heads"),
        ),
        check_vma=False,
    )
```

```python
import math

import jax
import jax.numpy as jnp
from jax import lax
from jax.sharding import PartitionSpec as P

D = 1024
DH = 64
TILE = 128
CAP = 1


norm_eps = 1e-05


def silu_slope(value):
    sigma = jax.nn.sigmoid(value)
    return sigma * (1.0 + value * (1.0 - sigma))


def route_tables(arrival_slot, owner_index, groups, per_owner):
    placed = arrival_slot.reshape(groups, per_owner)
    owners = placed // per_owner
    tile_ids = jnp.arange(per_owner, dtype=jnp.int32)
    same_owner = owners[:, :, None] == owners[:, None, :]
    earlier = tile_ids[None, :] < tile_ids[:, None]
    ranks = jnp.sum((same_owner & earlier[None, :, :]).astype(jnp.int32), axis=2)
    my_owners = lax.dynamic_index_in_dim(owners, owner_index, 0, keepdims=False)
    my_ranks = lax.dynamic_index_in_dim(ranks, owner_index, 0, keepdims=False)
    buffer_ids = jnp.arange(groups * CAP, dtype=jnp.int32)
    peers = buffer_ids // CAP
    turns = buffer_ids % CAP
    chosen = (my_owners[None, :] == peers[:, None]) & (my_ranks[None, :] == turns[:, None])
    send_index = jnp.sum(chosen.astype(jnp.int32) * tile_ids[None, :], axis=1)
    send_valid = jnp.any(chosen, axis=1)
    codes = (jnp.arange(groups, dtype=jnp.int32)[:, None] * CAP + ranks).reshape(-1)
    wanted = owner_index * per_owner + tile_ids
    matches = placed.reshape(-1)[None, :] == wanted[:, None]
    receive_index = jnp.sum(matches.astype(jnp.int32) * codes[None, :], axis=1)
    owner_lines = jnp.repeat(owners, CAP, axis=0)
    rank_lines = jnp.repeat(ranks, CAP, axis=0)
    place_lines = jnp.repeat(placed, CAP, axis=0)
    returning = (owner_lines == owner_index) & (rank_lines == turns[:, None])
    back_index = jnp.sum(
        returning.astype(jnp.int32) * (place_lines - owner_index * per_owner), axis=1
    )
    back_valid = jnp.any(returning, axis=1)
    home_index = my_owners * CAP + my_ranks
    return (send_index, send_valid, receive_index, back_index, back_valid, home_index)


def select_tiles(tiles, index, keep):
    del keep
    return jnp.take(tiles, index, axis=0)


def per_device(tokens, cotangent, gain, w_proj, w_out, arrival_slot, user_start, user_length):
    groups = lax.axis_size("users")
    owner_index = lax.axis_index("users")
    rows, width = tokens.shape
    per_owner = rows // TILE
    heads_here = w_proj.shape[1]
    scale = DH ** (-0.5)
    send_index, send_valid, receive_index, back_index, back_valid, home_index = route_tables(
        arrival_slot, owner_index, groups, per_owner
    )
    local_both = jnp.stack(
        [tokens.reshape(per_owner, TILE, width), cotangent.reshape(per_owner, TILE, width)], axis=1
    )
    arrived = lax.all_to_all(
        select_tiles(local_both, send_index, send_valid),
        "users",
        split_axis=0,
        concat_axis=0,
        tiled=True,
    )
    own_both = jnp.take(arrived, receive_index, axis=0)
    own_tokens = own_both[:, 0].reshape(rows, width)
    own_cotangent = own_both[:, 1].reshape(rows, width)
    full_both = lax.all_gather(own_both, "heads", axis=3, tiled=True)
    full_tokens = full_both[:, 0].reshape(rows, -1)
    full_cotangent = full_both[:, 1].reshape(rows, -1)
    tokens_wide = full_tokens.astype(jnp.float32)
    inv_rms = lax.rsqrt(jnp.mean(tokens_wide * tokens_wide, axis=1, keepdims=True) + norm_eps)
    normed = (tokens_wide * inv_rms * gain[None, :]).astype(jnp.bfloat16)
    proj_matrix = w_proj.reshape(w_proj.shape[0], heads_here * 4 * DH)
    projected = jnp.dot(normed, proj_matrix, preferred_element_type=jnp.float32).reshape(
        rows, heads_here, 4, DH
    )
    gate_rows = jax.nn.silu(projected[:, :, 0]).astype(jnp.bfloat16)
    value_rows = projected[:, :, 1].astype(jnp.bfloat16)
    query_rows = jax.nn.silu(projected[:, :, 2]).astype(jnp.bfloat16)
    key_rows = jax.nn.silu(projected[:, :, 3]).astype(jnp.bfloat16)
    grad_mix = (
        jnp.dot(full_cotangent, w_out.T, preferred_element_type=jnp.float32)
        .astype(jnp.bfloat16)
        .reshape(rows, heads_here, DH)
    )
    row_ids = jnp.arange(rows, dtype=jnp.int32)
    first = jnp.repeat(user_start, TILE)
    length = jnp.repeat(user_length, TILE)
    position = (row_ids // TILE - first) * TILE + row_ids % TILE
    is_live = position < length
    length_wide = length.astype(jnp.float32)
    blocks = 1
    mixer_parts = []
    grad_parts = []
    for head in range(heads_here):
        query_h = query_rows[:, head]
        key_h = key_rows[:, head]
        value_h = value_rows[:, head]
        gate_h = gate_rows[:, head]
        grad_mix_h = grad_mix[:, head]

        def block_step(carry, block):
            grad_key_sum, grad_value_sum = carry
            allowed = (
                (first[:, None] == first[None, :])
                & (position[None, :] <= position[:, None])
                & is_live[:, None]
                & is_live[None, :]
            )
            length_b = length_wide[:, None]
            scores = jnp.dot(query_h, key_h.T, preferred_element_type=jnp.float32) * scale
            weights = jnp.where(allowed, jax.nn.silu(scores) / length_b, 0.0).astype(jnp.bfloat16)
            attended = jnp.dot(weights, value_h, preferred_element_type=jnp.float32)
            inv_attn = lax.rsqrt(jnp.mean(attended * attended, axis=1, keepdims=True) + norm_eps)
            attn_normed = attended * inv_attn
            gate_wide = gate_h.astype(jnp.float32)
            grad_mix_wide = grad_mix_h.astype(jnp.float32)
            mixer_b = (attn_normed * gate_wide).astype(jnp.bfloat16)
            grad_gate_b = grad_mix_wide * attn_normed
            grad_attn_normed = grad_mix_wide * gate_wide
            grad_attended = (
                inv_attn
                * (
                    grad_attn_normed
                    - attn_normed * jnp.mean(grad_attn_normed * attn_normed, axis=1, keepdims=True)
                )
            ).astype(jnp.bfloat16)
            grad_weights = jnp.dot(grad_attended, value_h.T, preferred_element_type=jnp.float32)
            grad_scores = jnp.where(
                allowed, grad_weights / length_b * silu_slope(scores), 0.0
            ).astype(jnp.bfloat16)
            grad_query_b = jnp.dot(grad_scores, key_h, preferred_element_type=jnp.float32) * scale
            grad_key_sum = (
                grad_key_sum
                + jnp.dot(grad_scores.T, query_h, preferred_element_type=jnp.float32) * scale
            )
            grad_value_sum = grad_value_sum + jnp.dot(
                weights.T, grad_attended, preferred_element_type=jnp.float32
            )
            return ((grad_key_sum, grad_value_sum), (mixer_b, grad_gate_b, grad_query_b))

        start_sums = (jnp.zeros((rows, DH), jnp.float32), jnp.zeros((rows, DH), jnp.float32))
        (grad_key, grad_value), stacked = lax.scan(block_step, start_sums, jnp.arange(blocks))
        mixer_h = stacked[0].reshape(rows, DH)
        grad_gate = stacked[1].reshape(rows, DH)
        grad_query = stacked[2].reshape(rows, DH)
        mixer_h, grad_gate, grad_query, grad_key, grad_value = (
            mixer_h,
            grad_gate,
            grad_query,
            grad_key,
            grad_value,
        )
        before_act = projected[:, head]
        mixer_parts.append(mixer_h)
        grad_parts.append(
            jnp.stack(
                [
                    grad_gate * silu_slope(before_act[:, 0]),
                    grad_value,
                    grad_query * silu_slope(before_act[:, 2]),
                    grad_key * silu_slope(before_act[:, 3]),
                ],
                axis=1,
            )
        )
    mixer = jnp.concatenate(mixer_parts, axis=1)
    grad_proj = (
        jnp.stack(grad_parts, axis=1).astype(jnp.bfloat16).reshape(rows, heads_here * 4 * DH)
    )
    own_wide = own_tokens.astype(jnp.float32)
    heads_count = lax.axis_size("heads")
    mix_partial = jnp.einsum(
        "rk,khf->hrf",
        mixer,
        w_out.reshape(w_out.shape[0], heads_count, width),
        preferred_element_type=jnp.float32,
    )
    out_term = jnp.dot(full_cotangent.T, mixer, preferred_element_type=jnp.float32)
    proj_term = jnp.dot(normed.T, grad_proj, preferred_element_type=jnp.float32).reshape(
        normed.shape[1], heads_here, 4 * DH
    )
    normed_partial = jnp.einsum(
        "rk,hfk->hrf",
        grad_proj,
        proj_matrix.reshape(heads_count, width, proj_matrix.shape[1]),
        preferred_element_type=jnp.float32,
    )
    partial_totals = jnp.sum(
        grad_proj.astype(jnp.float32) * projected.reshape(rows, -1), axis=1
    ) / inv_rms[:, 0]
    extra = -(-rows // width)
    partial_totals = jnp.pad(partial_totals, (0, extra * width - rows)).reshape(1, extra, width)
    reduced = lax.psum_scatter(
        jnp.concatenate(
            [
                normed_partial,
                jnp.broadcast_to(partial_totals, (heads_count, extra, width)),
                mix_partial,
            ],
            axis=1,
        ).astype(jnp.bfloat16),
        "heads",
        scatter_dimension=0,
        tiled=True,
    ).astype(jnp.float32)
    grad_normed = reduced[0, :rows]
    row_totals = reduced[0, rows : rows + extra].reshape(-1)[:rows]
    mixed_own = (own_wide + reduced[0, rows + extra :]).astype(jnp.bfloat16)
    gain_share = lax.dynamic_slice_in_dim(gain, lax.axis_index("heads") * width, width)
    grad_scaled = grad_normed * gain_share[None, :]
    input_own = (
        own_cotangent.astype(jnp.float32)
        + inv_rms * grad_scaled
        - own_wide * (inv_rms * inv_rms * inv_rms) * (row_totals / D)[:, None]
    ).astype(jnp.bfloat16)
    norm_factor = 1.0 / math.sqrt(groups * rows)
    proj_cols = heads_here * 4 * DH
    weight_terms = jnp.concatenate(
        [proj_term.reshape(normed.shape[1], proj_cols), out_term], axis=1
    ).reshape(groups, normed.shape[1] // groups, proj_cols + out_term.shape[1])
    weight_sums = jnp.sum(
        lax.all_to_all(
            weight_terms.astype(jnp.bfloat16), "users", split_axis=0, concat_axis=0, tiled=True
        ).astype(jnp.float32),
        axis=0,
    )
    proj_sum = weight_sums[:, :proj_cols].reshape(-1, heads_here, 4 * DH)
    out_sum = weight_sums[:, proj_cols:]
    owned_both = jnp.stack(
        [mixed_own.reshape(per_owner, TILE, width), input_own.reshape(per_owner, TILE, width)],
        axis=1,
    )
    home = lax.all_to_all(
        select_tiles(owned_both, back_index, back_valid),
        "users",
        split_axis=0,
        concat_axis=0,
        tiled=True,
    )
    mixed = jnp.take(home[:, 0], home_index, axis=0).reshape(rows, width)
    input_grad = jnp.take(home[:, 1], home_index, axis=0).reshape(rows, width)
    return (mixed, input_grad, proj_sum * norm_factor, out_sum * norm_factor)


def solution(mesh):
    placed = (
        P("users", "heads"),
        P("users", "heads"),
        P(),
        P(None, "heads", None),
        P("heads", None),
        P(),
        P("users"),
        P("users"),
    )
    return jax.shard_map(
        per_device,
        mesh=mesh,
        in_specs=placed,
        out_specs=(
            P("users", "heads"),
            P("users", "heads"),
            P("users", "heads", None),
            P("users", "heads"),
        ),
        check_vma=False,
    )
```

```python
import math

import jax
import jax.numpy as jnp
from jax import lax
from jax.sharding import PartitionSpec as P

D = 1024
DH = 64
TILE = 128
CAP = 1


norm_eps = 1e-05


def silu_slope(value):
    sigma = jax.nn.sigmoid(value)
    return sigma * (1.0 + value * (1.0 - sigma))


def route_tables(arrival_slot, owner_index, groups, per_owner):
    placed = arrival_slot.reshape(groups, per_owner)
    owners = placed // per_owner
    tile_ids = jnp.arange(per_owner, dtype=jnp.int32)
    same_owner = owners[:, :, None] == owners[:, None, :]
    earlier = tile_ids[None, :] < tile_ids[:, None]
    ranks = jnp.sum((same_owner & earlier[None, :, :]).astype(jnp.int32), axis=2)
    my_owners = lax.dynamic_index_in_dim(owners, owner_index, 0, keepdims=False)
    my_ranks = lax.dynamic_index_in_dim(ranks, owner_index, 0, keepdims=False)
    buffer_ids = jnp.arange(groups * CAP, dtype=jnp.int32)
    peers = buffer_ids // CAP
    turns = buffer_ids % CAP
    chosen = (my_owners[None, :] == peers[:, None]) & (my_ranks[None, :] == turns[:, None])
    send_index = jnp.sum(chosen.astype(jnp.int32) * tile_ids[None, :], axis=1)
    send_valid = jnp.any(chosen, axis=1)
    codes = (jnp.arange(groups, dtype=jnp.int32)[:, None] * CAP + ranks).reshape(-1)
    wanted = owner_index * per_owner + tile_ids
    matches = placed.reshape(-1)[None, :] == wanted[:, None]
    receive_index = jnp.sum(matches.astype(jnp.int32) * codes[None, :], axis=1)
    owner_lines = jnp.repeat(owners, CAP, axis=0)
    rank_lines = jnp.repeat(ranks, CAP, axis=0)
    place_lines = jnp.repeat(placed, CAP, axis=0)
    returning = (owner_lines == owner_index) & (rank_lines == turns[:, None])
    back_index = jnp.sum(
        returning.astype(jnp.int32) * (place_lines - owner_index * per_owner), axis=1
    )
    back_valid = jnp.any(returning, axis=1)
    home_index = my_owners * CAP + my_ranks
    return (send_index, send_valid, receive_index, back_index, back_valid, home_index)


def select_tiles(tiles, index, keep):
    del keep
    return jnp.take(tiles, index, axis=0, mode="clip")


def per_device(tokens, cotangent, gain, w_proj, w_out, arrival_slot, user_start, user_length):
    groups = lax.axis_size("users")
    owner_index = lax.axis_index("users")
    rows, width = tokens.shape
    per_owner = rows // TILE
    heads_here = w_proj.shape[1]
    scale = DH ** (-0.5)
    send_index, send_valid, receive_index, back_index, back_valid, home_index = route_tables(
        arrival_slot, owner_index, groups, per_owner
    )
    local_both = jnp.stack(
        [tokens.reshape(per_owner, TILE, width), cotangent.reshape(per_owner, TILE, width)], axis=1
    )
    arrived = lax.all_to_all(
        select_tiles(local_both, send_index, send_valid),
        "users",
        split_axis=0,
        concat_axis=0,
        tiled=True,
    )
    own_both = jnp.take(arrived, receive_index, axis=0, mode="clip")
    own_tokens = own_both[:, 0].reshape(rows, width)
    own_cotangent = own_both[:, 1].reshape(rows, width)
    full_both = lax.all_gather(own_both, "heads", axis=3, tiled=True)
    full_tokens = full_both[:, 0].reshape(rows, -1)
    full_cotangent = full_both[:, 1].reshape(rows, -1)
    tokens_wide = full_tokens.astype(jnp.float32)
    inv_rms = lax.rsqrt(jnp.mean(tokens_wide * tokens_wide, axis=1, keepdims=True) + norm_eps)
    normed = (tokens_wide * inv_rms * gain[None, :]).astype(jnp.bfloat16)
    proj_matrix = w_proj.reshape(w_proj.shape[0], heads_here * 4 * DH)
    projected = jnp.dot(normed, proj_matrix, preferred_element_type=jnp.float32).reshape(
        rows, heads_here, 4, DH
    )
    gate_rows = jax.nn.silu(projected[:, :, 0]).astype(jnp.bfloat16)
    value_rows = projected[:, :, 1].astype(jnp.bfloat16)
    query_rows = jax.nn.silu(projected[:, :, 2]).astype(jnp.bfloat16)
    key_rows = jax.nn.silu(projected[:, :, 3]).astype(jnp.bfloat16)
    grad_mix = (
        jnp.dot(full_cotangent, w_out.T, preferred_element_type=jnp.float32)
        .astype(jnp.bfloat16)
        .reshape(rows, heads_here, DH)
    )
    row_ids = jnp.arange(rows, dtype=jnp.int32)
    first = jnp.repeat(user_start, TILE)
    length = jnp.repeat(user_length, TILE)
    position = (row_ids // TILE - first) * TILE + row_ids % TILE
    is_live = position < length
    length_wide = length.astype(jnp.float32)
    blocks = 1
    mixer_parts = []
    grad_parts = []
    for head in range(heads_here):
        query_h = query_rows[:, head]
        key_h = key_rows[:, head]
        value_h = value_rows[:, head]
        gate_h = gate_rows[:, head]
        grad_mix_h = grad_mix[:, head]

        def block_step(carry, block):
            grad_key_sum, grad_value_sum = carry
            allowed = (
                (first[:, None] == first[None, :])
                & (position[None, :] <= position[:, None])
                & is_live[:, None]
                & is_live[None, :]
            )
            length_b = length_wide[:, None]
            scores = jnp.dot(query_h, key_h.T, preferred_element_type=jnp.float32) * scale
            weights = jnp.where(allowed, jax.nn.silu(scores) / length_b, 0.0).astype(jnp.bfloat16)
            attended = jnp.dot(weights, value_h, preferred_element_type=jnp.float32)
            inv_attn = lax.rsqrt(jnp.mean(attended * attended, axis=1, keepdims=True) + norm_eps)
            attn_normed = attended * inv_attn
            gate_wide = gate_h.astype(jnp.float32)
            grad_mix_wide = grad_mix_h.astype(jnp.float32)
            mixer_b = (attn_normed * gate_wide).astype(jnp.bfloat16)
            grad_gate_b = grad_mix_wide * attn_normed
            grad_attn_normed = grad_mix_wide * gate_wide
            grad_attended = (
                inv_attn
                * (
                    grad_attn_normed
                    - attn_normed * jnp.mean(grad_attn_normed * attn_normed, axis=1, keepdims=True)
                )
            ).astype(jnp.bfloat16)
            grad_weights = jnp.dot(grad_attended, value_h.T, preferred_element_type=jnp.float32)
            grad_scores = jnp.where(
                allowed, grad_weights / length_b * silu_slope(scores), 0.0
            ).astype(jnp.bfloat16)
            grad_query_b = jnp.dot(grad_scores, key_h, preferred_element_type=jnp.float32) * scale
            grad_key_sum = (
                grad_key_sum
                + jnp.dot(grad_scores.T, query_h, preferred_element_type=jnp.float32) * scale
            )
            grad_value_sum = grad_value_sum + jnp.dot(
                weights.T, grad_attended, preferred_element_type=jnp.float32
            )
            return ((grad_key_sum, grad_value_sum), (mixer_b, grad_gate_b, grad_query_b))

        start_sums = (jnp.zeros((rows, DH), jnp.float32), jnp.zeros((rows, DH), jnp.float32))
        (grad_key, grad_value), stacked = lax.scan(block_step, start_sums, jnp.arange(blocks))
        mixer_h = stacked[0].reshape(rows, DH)
        grad_gate = stacked[1].reshape(rows, DH)
        grad_query = stacked[2].reshape(rows, DH)
        mixer_h, grad_gate, grad_query, grad_key, grad_value = (
            mixer_h,
            grad_gate,
            grad_query,
            grad_key,
            grad_value,
        )
        before_act = projected[:, head]
        mixer_parts.append(mixer_h)
        grad_parts.append(
            jnp.stack(
                [
                    grad_gate * silu_slope(before_act[:, 0]),
                    grad_value,
                    grad_query * silu_slope(before_act[:, 2]),
                    grad_key * silu_slope(before_act[:, 3]),
                ],
                axis=1,
            )
        )
    mixer = jnp.concatenate(mixer_parts, axis=1)
    grad_proj = (
        jnp.stack(grad_parts, axis=1).astype(jnp.bfloat16).reshape(rows, heads_here * 4 * DH)
    )
    own_wide = own_tokens.astype(jnp.float32)
    heads_count = lax.axis_size("heads")
    mix_partial = jnp.einsum(
        "rk,khf->hrf",
        mixer,
        w_out.reshape(w_out.shape[0], heads_count, width),
        preferred_element_type=jnp.float32,
    )
    out_term = jnp.dot(full_cotangent.T, mixer, preferred_element_type=jnp.float32)
    proj_term = jnp.dot(normed.T, grad_proj, preferred_element_type=jnp.float32).reshape(
        normed.shape[1], heads_here, 4 * DH
    )
    normed_partial = jnp.einsum(
        "rk,hfk->hrf",
        grad_proj,
        proj_matrix.reshape(heads_count, width, proj_matrix.shape[1]),
        preferred_element_type=jnp.float32,
    )
    partial_totals = jnp.sum(
        grad_proj.astype(jnp.float32) * projected.reshape(rows, -1), axis=1
    ) / inv_rms[:, 0]
    extra = -(-rows // width)
    partial_totals = jnp.pad(partial_totals, (0, extra * width - rows)).reshape(1, extra, width)
    reduced = lax.psum_scatter(
        jnp.concatenate(
            [
                normed_partial,
                jnp.broadcast_to(partial_totals, (heads_count, extra, width)),
                mix_partial,
            ],
            axis=1,
        ).astype(jnp.bfloat16),
        "heads",
        scatter_dimension=0,
        tiled=True,
    ).astype(jnp.float32)
    grad_normed = reduced[0, :rows]
    row_totals = reduced[0, rows : rows + extra].reshape(-1)[:rows]
    mixed_own = (own_wide + reduced[0, rows + extra :]).astype(jnp.bfloat16)
    gain_share = lax.dynamic_slice_in_dim(gain, lax.axis_index("heads") * width, width)
    grad_scaled = grad_normed * gain_share[None, :]
    input_own = (
        own_cotangent.astype(jnp.float32)
        + inv_rms * grad_scaled
        - own_wide * (inv_rms * inv_rms * inv_rms) * (row_totals / D)[:, None]
    ).astype(jnp.bfloat16)
    norm_factor = 1.0 / math.sqrt(groups * rows)
    proj_cols = heads_here * 4 * DH
    weight_terms = jnp.concatenate(
        [proj_term.reshape(normed.shape[1], proj_cols), out_term], axis=1
    ).reshape(groups, normed.shape[1] // groups, proj_cols + out_term.shape[1])
    weight_sums = jnp.sum(
        lax.all_to_all(
            weight_terms.astype(jnp.bfloat16), "users", split_axis=0, concat_axis=0, tiled=True
        ).astype(jnp.float32),
        axis=0,
    )
    proj_sum = weight_sums[:, :proj_cols].reshape(-1, heads_here, 4 * DH)
    out_sum = weight_sums[:, proj_cols:]
    owned_both = jnp.stack(
        [mixed_own.reshape(per_owner, TILE, width), input_own.reshape(per_owner, TILE, width)],
        axis=1,
    )
    home = lax.all_to_all(
        select_tiles(owned_both, back_index, back_valid),
        "users",
        split_axis=0,
        concat_axis=0,
        tiled=True,
    )
    mixed = jnp.take(home[:, 0], home_index, axis=0, mode="clip").reshape(rows, width)
    input_grad = jnp.take(home[:, 1], home_index, axis=0, mode="clip").reshape(rows, width)
    return (mixed, input_grad, proj_sum * norm_factor, out_sum * norm_factor)


def solution(mesh):
    placed = (
        P("users", "heads"),
        P("users", "heads"),
        P(),
        P(None, "heads", None),
        P("heads", None),
        P(),
        P("users"),
        P("users"),
    )
    return jax.shard_map(
        per_device,
        mesh=mesh,
        in_specs=placed,
        out_specs=(
            P("users", "heads"),
            P("users", "heads"),
            P("users", "heads", None),
            P("users", "heads"),
        ),
        check_vma=False,
    )
```

```python
import math

import jax
import jax.numpy as jnp
from jax import lax
from jax.sharding import PartitionSpec as P

D = 1024
DH = 64
TILE = 128
CAP = 1


norm_eps = 1e-05


def silu_slope(value):
    sigma = jax.nn.sigmoid(value)
    return sigma * (1.0 + value * (1.0 - sigma))


def route_tables(arrival_slot, owner_index, groups, per_owner):
    placed = arrival_slot.reshape(groups, per_owner)
    owners = placed // per_owner
    tile_ids = jnp.arange(per_owner, dtype=jnp.int32)
    same_owner = owners[:, :, None] == owners[:, None, :]
    earlier = tile_ids[None, :] < tile_ids[:, None]
    ranks = jnp.sum((same_owner & earlier[None, :, :]).astype(jnp.int32), axis=2)
    my_owners = lax.dynamic_index_in_dim(owners, owner_index, 0, keepdims=False)
    my_ranks = lax.dynamic_index_in_dim(ranks, owner_index, 0, keepdims=False)
    buffer_ids = jnp.arange(groups * CAP, dtype=jnp.int32)
    peers = buffer_ids // CAP
    turns = buffer_ids % CAP
    chosen = (my_owners[None, :] == peers[:, None]) & (my_ranks[None, :] == turns[:, None])
    send_index = jnp.sum(chosen.astype(jnp.int32) * tile_ids[None, :], axis=1)
    send_valid = jnp.any(chosen, axis=1)
    codes = (jnp.arange(groups, dtype=jnp.int32)[:, None] * CAP + ranks).reshape(-1)
    wanted = owner_index * per_owner + tile_ids
    matches = placed.reshape(-1)[None, :] == wanted[:, None]
    receive_index = jnp.sum(matches.astype(jnp.int32) * codes[None, :], axis=1)
    owner_lines = jnp.repeat(owners, CAP, axis=0)
    rank_lines = jnp.repeat(ranks, CAP, axis=0)
    place_lines = jnp.repeat(placed, CAP, axis=0)
    returning = (owner_lines == owner_index) & (rank_lines == turns[:, None])
    back_index = jnp.sum(
        returning.astype(jnp.int32) * (place_lines - owner_index * per_owner), axis=1
    )
    back_valid = jnp.any(returning, axis=1)
    home_index = my_owners * CAP + my_ranks
    return (send_index, send_valid, receive_index, back_index, back_valid, home_index)


def select_tiles(tiles, index, keep):
    del keep
    return jnp.take(tiles, index, axis=0, mode="clip")


def per_device(tokens, cotangent, gain, w_proj, w_out, arrival_slot, user_start, user_length):
    groups = lax.axis_size("users")
    owner_index = lax.axis_index("users")
    rows, width = tokens.shape
    per_owner = rows // TILE
    heads_here = w_proj.shape[1]
    scale = DH ** (-0.5)
    send_index, send_valid, receive_index, back_index, back_valid, home_index = route_tables(
        arrival_slot, owner_index, groups, per_owner
    )
    local_both = jnp.stack(
        [tokens.reshape(per_owner, TILE, width), cotangent.reshape(per_owner, TILE, width)], axis=1
    )
    arrived = lax.all_to_all(
        select_tiles(local_both, send_index, send_valid),
        "users",
        split_axis=0,
        concat_axis=0,
        tiled=True,
    )
    own_both = jnp.take(arrived, receive_index, axis=0, mode="clip")
    own_tokens = own_both[:, 0].reshape(rows, width)
    own_cotangent = own_both[:, 1].reshape(rows, width)
    full_both = lax.all_gather(own_both, "heads", axis=3, tiled=True)
    full_tokens = full_both[:, 0].reshape(rows, -1)
    full_cotangent = full_both[:, 1].reshape(rows, -1)
    tokens_wide = full_tokens.astype(jnp.float32)
    inv_rms = lax.rsqrt(jnp.mean(tokens_wide * tokens_wide, axis=1, keepdims=True) + norm_eps)
    normed = (tokens_wide * inv_rms * gain[None, :]).astype(jnp.bfloat16)
    proj_matrix = w_proj.reshape(w_proj.shape[0], heads_here * 4 * DH)
    projected = jnp.dot(normed, proj_matrix, preferred_element_type=jnp.float32).reshape(
        rows, heads_here, 4, DH
    )
    gate_rows = jax.nn.silu(projected[:, :, 0]).astype(jnp.bfloat16)
    value_rows = projected[:, :, 1].astype(jnp.bfloat16)
    query_rows = jax.nn.silu(projected[:, :, 2]).astype(jnp.bfloat16)
    key_rows = jax.nn.silu(projected[:, :, 3]).astype(jnp.bfloat16)
    grad_mix = (
        jnp.dot(full_cotangent, w_out.T, preferred_element_type=jnp.float32)
        .astype(jnp.bfloat16)
        .reshape(rows, heads_here, DH)
    )
    row_ids = jnp.arange(rows, dtype=jnp.int32)
    first = jnp.repeat(user_start, TILE)
    length = jnp.repeat(user_length, TILE)
    position = (row_ids // TILE - first) * TILE + row_ids % TILE
    is_live = position < length
    length_wide = length.astype(jnp.float32)
    blocks = 1
    mixer_parts = []
    grad_parts = []
    for head in range(heads_here):
        query_h = query_rows[:, head]
        key_h = key_rows[:, head]
        value_h = value_rows[:, head]
        gate_h = gate_rows[:, head]
        grad_mix_h = grad_mix[:, head]

        def block_step(carry, block):
            grad_key_sum, grad_value_sum = carry
            allowed = (
                (first[:, None] == first[None, :])
                & (position[None, :] <= position[:, None])
                & is_live[:, None]
                & is_live[None, :]
            )
            length_b = length_wide[:, None]
            scores = jnp.dot(query_h, key_h.T, preferred_element_type=jnp.float32) * scale
            weights = jnp.where(allowed, jax.nn.silu(scores) / length_b, 0.0).astype(jnp.bfloat16)
            attended = jnp.dot(weights, value_h, preferred_element_type=jnp.float32)
            inv_attn = lax.rsqrt(jnp.mean(attended * attended, axis=1, keepdims=True) + norm_eps)
            attn_normed = attended * inv_attn
            gate_wide = gate_h.astype(jnp.float32)
            grad_mix_wide = grad_mix_h.astype(jnp.float32)
            mixer_b = (attn_normed * gate_wide).astype(jnp.bfloat16)
            grad_gate_b = grad_mix_wide * attn_normed
            grad_attn_normed = grad_mix_wide * gate_wide
            grad_attended = (
                inv_attn
                * (
                    grad_attn_normed
                    - attn_normed * jnp.mean(grad_attn_normed * attn_normed, axis=1, keepdims=True)
                )
            ).astype(jnp.bfloat16)
            grad_weights = jnp.dot(grad_attended, value_h.T, preferred_element_type=jnp.float32)
            grad_scores = jnp.where(
                allowed, grad_weights / length_b * silu_slope(scores), 0.0
            ).astype(jnp.bfloat16)
            grad_query_b = jnp.dot(grad_scores, key_h, preferred_element_type=jnp.float32) * scale
            grad_key_sum = (
                grad_key_sum
                + jnp.dot(grad_scores.T, query_h, preferred_element_type=jnp.float32) * scale
            )
            grad_value_sum = grad_value_sum + jnp.dot(
                weights.T, grad_attended, preferred_element_type=jnp.float32
            )
            return ((grad_key_sum, grad_value_sum), (mixer_b, grad_gate_b, grad_query_b))

        start_sums = (jnp.zeros((rows, DH), jnp.float32), jnp.zeros((rows, DH), jnp.float32))
        (grad_key, grad_value), stacked = lax.scan(block_step, start_sums, jnp.arange(blocks))
        mixer_h = stacked[0].reshape(rows, DH)
        grad_gate = stacked[1].reshape(rows, DH)
        grad_query = stacked[2].reshape(rows, DH)
        mixer_h, grad_gate, grad_query, grad_key, grad_value = (
            mixer_h,
            grad_gate,
            grad_query,
            grad_key,
            grad_value,
        )
        before_act = projected[:, head]
        mixer_parts.append(mixer_h)
        grad_parts.append(
            jnp.stack(
                [
                    grad_gate * silu_slope(before_act[:, 0]),
                    grad_value,
                    grad_query * silu_slope(before_act[:, 2]),
                    grad_key * silu_slope(before_act[:, 3]),
                ],
                axis=1,
            )
        )
    mixer = jnp.concatenate(mixer_parts, axis=1)
    grad_proj = (
        jnp.stack(grad_parts, axis=1).astype(jnp.bfloat16).reshape(rows, heads_here * 4 * DH)
    )
    own_wide = own_tokens.astype(jnp.float32)
    heads_count = lax.axis_size("heads")
    mix_partial = jnp.einsum(
        "rk,khf->hrf",
        mixer,
        w_out.reshape(w_out.shape[0], heads_count, width),
        preferred_element_type=jnp.float32,
    )
    out_term = jnp.dot(full_cotangent.T, mixer, preferred_element_type=jnp.float32)
    proj_term = jnp.dot(normed.T, grad_proj, preferred_element_type=jnp.float32).reshape(
        normed.shape[1], heads_here, 4 * DH
    )
    normed_partial = jnp.einsum(
        "rk,hfk->hrf",
        grad_proj,
        proj_matrix.reshape(heads_count, width, proj_matrix.shape[1]),
        preferred_element_type=jnp.float32,
    )
    partial_totals = jnp.sum(
        grad_proj.astype(jnp.float32) * projected.reshape(rows, -1), axis=1
    ) / inv_rms[:, 0]
    extra = -(-rows // width)
    partial_totals = jnp.pad(partial_totals, (0, extra * width - rows)).reshape(1, extra, width)
    reduced = lax.psum_scatter(
        jnp.concatenate(
            [
                normed_partial,
                jnp.broadcast_to(partial_totals, (heads_count, extra, width)),
            ],
            axis=1,
        ).astype(jnp.bfloat16),
        "heads",
        scatter_dimension=0,
        tiled=True,
    ).astype(jnp.float32)
    grad_normed = reduced[0, :rows]
    row_totals = reduced[0, rows : rows + extra].reshape(-1)[:rows]
    mix_share = jnp.sum(
        lax.all_to_all(
            mix_partial.astype(jnp.bfloat16), "heads", split_axis=0, concat_axis=0, tiled=True
        ).astype(jnp.float32),
        axis=0,
    )
    mixed_own = (own_wide + mix_share).astype(jnp.bfloat16)
    gain_share = lax.dynamic_slice_in_dim(gain, lax.axis_index("heads") * width, width)
    grad_scaled = grad_normed * gain_share[None, :]
    input_own = (
        own_cotangent.astype(jnp.float32)
        + inv_rms * grad_scaled
        - own_wide * (inv_rms * inv_rms * inv_rms) * (row_totals / D)[:, None]
    ).astype(jnp.bfloat16)
    norm_factor = 1.0 / math.sqrt(groups * rows)
    proj_cols = heads_here * 4 * DH
    weight_terms = jnp.concatenate(
        [proj_term.reshape(normed.shape[1], proj_cols), out_term], axis=1
    ).reshape(groups, normed.shape[1] // groups, proj_cols + out_term.shape[1])
    weight_sums = jnp.sum(
        lax.all_to_all(
            weight_terms.astype(jnp.bfloat16), "users", split_axis=0, concat_axis=0, tiled=True
        ).astype(jnp.float32),
        axis=0,
    )
    proj_sum = weight_sums[:, :proj_cols].reshape(-1, heads_here, 4 * DH)
    out_sum = weight_sums[:, proj_cols:]
    owned_both = jnp.stack(
        [mixed_own.reshape(per_owner, TILE, width), input_own.reshape(per_owner, TILE, width)],
        axis=1,
    )
    home = lax.all_to_all(
        select_tiles(owned_both, back_index, back_valid),
        "users",
        split_axis=0,
        concat_axis=0,
        tiled=True,
    )
    mixed = jnp.take(home[:, 0], home_index, axis=0, mode="clip").reshape(rows, width)
    input_grad = jnp.take(home[:, 1], home_index, axis=0, mode="clip").reshape(rows, width)
    return (mixed, input_grad, proj_sum * norm_factor, out_sum * norm_factor)


def solution(mesh):
    placed = (
        P("users", "heads"),
        P("users", "heads"),
        P(),
        P(None, "heads", None),
        P("heads", None),
        P(),
        P("users"),
        P("users"),
    )
    return jax.shard_map(
        per_device,
        mesh=mesh,
        in_specs=placed,
        out_specs=(
            P("users", "heads"),
            P("users", "heads"),
            P("users", "heads", None),
            P("users", "heads"),
        ),
        check_vma=False,
    )
```

```python
import math

import jax
import jax.numpy as jnp
from jax import lax
from jax.sharding import PartitionSpec as P

D = 1024
DH = 64
TILE = 128
CAP = 1


norm_eps = 1e-05


def silu_slope(value):
    sigma = jax.nn.sigmoid(value)
    return sigma * (1.0 + value * (1.0 - sigma))


def route_tables(arrival_slot, owner_index, groups, per_owner):
    placed = arrival_slot.reshape(groups, per_owner)
    owners = placed // per_owner
    tile_ids = jnp.arange(per_owner, dtype=jnp.int32)
    same_owner = owners[:, :, None] == owners[:, None, :]
    earlier = tile_ids[None, :] < tile_ids[:, None]
    ranks = jnp.sum((same_owner & earlier[None, :, :]).astype(jnp.int32), axis=2)
    my_owners = lax.dynamic_index_in_dim(owners, owner_index, 0, keepdims=False)
    my_ranks = lax.dynamic_index_in_dim(ranks, owner_index, 0, keepdims=False)
    buffer_ids = jnp.arange(groups * CAP, dtype=jnp.int32)
    peers = buffer_ids // CAP
    turns = buffer_ids % CAP
    chosen = (my_owners[None, :] == peers[:, None]) & (my_ranks[None, :] == turns[:, None])
    send_index = jnp.sum(chosen.astype(jnp.int32) * tile_ids[None, :], axis=1)
    send_valid = jnp.any(chosen, axis=1)
    codes = (jnp.arange(groups, dtype=jnp.int32)[:, None] * CAP + ranks).reshape(-1)
    wanted = owner_index * per_owner + tile_ids
    matches = placed.reshape(-1)[None, :] == wanted[:, None]
    receive_index = jnp.sum(matches.astype(jnp.int32) * codes[None, :], axis=1)
    owner_lines = jnp.repeat(owners, CAP, axis=0)
    rank_lines = jnp.repeat(ranks, CAP, axis=0)
    place_lines = jnp.repeat(placed, CAP, axis=0)
    returning = (owner_lines == owner_index) & (rank_lines == turns[:, None])
    back_index = jnp.sum(
        returning.astype(jnp.int32) * (place_lines - owner_index * per_owner), axis=1
    )
    back_valid = jnp.any(returning, axis=1)
    home_index = my_owners * CAP + my_ranks
    return (send_index, send_valid, receive_index, back_index, back_valid, home_index)


def select_tiles(tiles, index, keep):
    del keep
    return jnp.take(tiles, index, axis=0, mode="clip")


def per_device(tokens, cotangent, gain, w_proj, w_out, arrival_slot, user_start, user_length):
    groups = lax.axis_size("users")
    owner_index = lax.axis_index("users")
    rows, width = tokens.shape
    per_owner = rows // TILE
    heads_here = w_proj.shape[1]
    scale = DH ** (-0.5)
    send_index, send_valid, receive_index, back_index, back_valid, home_index = route_tables(
        arrival_slot, owner_index, groups, per_owner
    )
    local_both = jnp.stack(
        [tokens.reshape(per_owner, TILE, width), cotangent.reshape(per_owner, TILE, width)], axis=1
    )
    arrived = lax.all_to_all(
        select_tiles(local_both, send_index, send_valid),
        "users",
        split_axis=0,
        concat_axis=0,
        tiled=True,
    )
    own_both = jnp.take(arrived, receive_index, axis=0, mode="clip")
    own_tokens = own_both[:, 0].reshape(rows, width)
    own_cotangent = own_both[:, 1].reshape(rows, width)
    full_both = lax.all_gather(own_both, "heads", axis=3, tiled=True)
    full_tokens = full_both[:, 0].reshape(rows, -1)
    full_cotangent = full_both[:, 1].reshape(rows, -1)
    tokens_wide = full_tokens.astype(jnp.float32)
    inv_rms = lax.rsqrt(jnp.mean(tokens_wide * tokens_wide, axis=1, keepdims=True) + norm_eps)
    normed = (tokens_wide * inv_rms * gain[None, :]).astype(jnp.bfloat16)
    proj_matrix = w_proj.reshape(w_proj.shape[0], heads_here * 4 * DH)
    projected = jnp.dot(normed, proj_matrix, preferred_element_type=jnp.float32).reshape(
        rows, heads_here, 4, DH
    )
    gate_rows = jax.nn.silu(projected[:, :, 0]).astype(jnp.bfloat16)
    value_rows = projected[:, :, 1].astype(jnp.bfloat16)
    query_rows = jax.nn.silu(projected[:, :, 2]).astype(jnp.bfloat16)
    key_rows = jax.nn.silu(projected[:, :, 3]).astype(jnp.bfloat16)
    grad_mix = (
        jnp.dot(full_cotangent, w_out.T, preferred_element_type=jnp.float32)
        .astype(jnp.bfloat16)
        .reshape(rows, heads_here, DH)
    )
    row_ids = jnp.arange(rows, dtype=jnp.int32)
    first = jnp.repeat(user_start, TILE)
    length = jnp.repeat(user_length, TILE)
    position = (row_ids // TILE - first) * TILE + row_ids % TILE
    is_live = position < length
    length_wide = length.astype(jnp.float32)
    blocks = 1
    mixer_parts = []
    grad_parts = []
    for head in range(heads_here):
        query_h = query_rows[:, head]
        key_h = key_rows[:, head]
        value_h = value_rows[:, head]
        gate_h = gate_rows[:, head]
        grad_mix_h = grad_mix[:, head]

        def block_step(carry, block):
            grad_key_sum, grad_value_sum = carry
            allowed = (
                (first[:, None] == first[None, :])
                & (position[None, :] <= position[:, None])
                & is_live[:, None]
                & is_live[None, :]
            )
            length_b = length_wide[:, None]
            scores = jnp.dot(query_h, key_h.T, preferred_element_type=jnp.float32) * scale
            weights = jnp.where(allowed, jax.nn.silu(scores) / length_b, 0.0).astype(jnp.bfloat16)
            attended = jnp.dot(weights, value_h, preferred_element_type=jnp.float32)
            inv_attn = lax.rsqrt(jnp.mean(attended * attended, axis=1, keepdims=True) + norm_eps)
            attn_normed = attended * inv_attn
            gate_wide = gate_h.astype(jnp.float32)
            grad_mix_wide = grad_mix_h.astype(jnp.float32)
            mixer_b = (attn_normed * gate_wide).astype(jnp.bfloat16)
            grad_gate_b = grad_mix_wide * attn_normed
            grad_attn_normed = grad_mix_wide * gate_wide
            grad_attended = (
                inv_attn
                * (
                    grad_attn_normed
                    - attn_normed * jnp.mean(grad_attn_normed * attn_normed, axis=1, keepdims=True)
                )
            ).astype(jnp.bfloat16)
            grad_weights = jnp.dot(grad_attended, value_h.T, preferred_element_type=jnp.float32)
            grad_scores = jnp.where(
                allowed, grad_weights / length_b * silu_slope(scores), 0.0
            ).astype(jnp.bfloat16)
            grad_query_b = jnp.dot(grad_scores, key_h, preferred_element_type=jnp.float32) * scale
            grad_key_sum = (
                grad_key_sum
                + jnp.dot(grad_scores.T, query_h, preferred_element_type=jnp.float32) * scale
            )
            grad_value_sum = grad_value_sum + jnp.dot(
                weights.T, grad_attended, preferred_element_type=jnp.float32
            )
            return ((grad_key_sum, grad_value_sum), (mixer_b, grad_gate_b, grad_query_b))

        start_sums = (jnp.zeros((rows, DH), jnp.float32), jnp.zeros((rows, DH), jnp.float32))
        (grad_key, grad_value), stacked = lax.scan(block_step, start_sums, jnp.arange(blocks))
        mixer_h = stacked[0].reshape(rows, DH)
        grad_gate = stacked[1].reshape(rows, DH)
        grad_query = stacked[2].reshape(rows, DH)
        mixer_h, grad_gate, grad_query, grad_key, grad_value = (
            mixer_h,
            grad_gate,
            grad_query,
            grad_key,
            grad_value,
        )
        before_act = projected[:, head]
        mixer_parts.append(mixer_h)
        grad_parts.append(
            jnp.stack(
                [
                    grad_gate * silu_slope(before_act[:, 0]),
                    grad_value,
                    grad_query * silu_slope(before_act[:, 2]),
                    grad_key * silu_slope(before_act[:, 3]),
                ],
                axis=1,
            )
        )
    mixer = jnp.concatenate(mixer_parts, axis=1)
    grad_proj = (
        jnp.stack(grad_parts, axis=1).astype(jnp.bfloat16).reshape(rows, heads_here * 4 * DH)
    )
    own_wide = own_tokens.astype(jnp.float32)
    heads_count = lax.axis_size("heads")
    mix_partial = jnp.einsum(
        "rk,khf->hrf",
        mixer,
        w_out.reshape(w_out.shape[0], heads_count, width),
        preferred_element_type=jnp.float32,
    )
    out_term = jnp.dot(full_cotangent.T, mixer, preferred_element_type=jnp.float32)
    proj_term = jnp.dot(normed.T, grad_proj, preferred_element_type=jnp.float32).reshape(
        normed.shape[1], heads_here, 4 * DH
    )
    normed_partial = jnp.einsum(
        "rk,hfk->hrf",
        grad_proj,
        proj_matrix.reshape(heads_count, width, proj_matrix.shape[1]),
        preferred_element_type=jnp.float32,
    )
    partial_totals = jnp.sum(
        grad_proj.astype(jnp.float32) * projected.reshape(rows, -1), axis=1
    ) / inv_rms[:, 0]
    extra = -(-rows // width)
    partial_totals = jnp.pad(partial_totals, (0, extra * width - rows)).reshape(1, extra, width)
    reduced = lax.psum_scatter(
        jnp.concatenate(
            [
                normed_partial,
                jnp.broadcast_to(partial_totals, (heads_count, extra, width)),
                mix_partial,
            ],
            axis=1,
        ).astype(jnp.bfloat16),
        "heads",
        scatter_dimension=0,
        tiled=True,
    ).astype(jnp.float32)
    grad_normed = reduced[0, :rows]
    row_totals = reduced[0, rows : rows + extra].reshape(-1)[:rows]
    mixed_own = (own_wide + reduced[0, rows + extra :]).astype(jnp.bfloat16)
    gain_share = lax.dynamic_slice_in_dim(gain, lax.axis_index("heads") * width, width)
    grad_scaled = grad_normed * gain_share[None, :]
    input_own = (
        own_cotangent.astype(jnp.float32)
        + inv_rms * grad_scaled
        - own_wide * (inv_rms * inv_rms * inv_rms) * (row_totals / D)[:, None]
    ).astype(jnp.bfloat16)
    norm_factor = 1.0 / math.sqrt(groups * rows)
    proj_cols = heads_here * 4 * DH
    weight_terms = jnp.concatenate(
        [proj_term.reshape(normed.shape[1], proj_cols), out_term], axis=1
    ).reshape(groups, normed.shape[1] // groups, proj_cols + out_term.shape[1])
    weight_sums = jnp.sum(
        lax.all_to_all(
            weight_terms.astype(jnp.bfloat16), "users", split_axis=0, concat_axis=0, tiled=True
        ).astype(jnp.float32),
        axis=0,
    )
    proj_sum = weight_sums[:, :proj_cols].reshape(-1, heads_here, 4 * DH)
    out_sum = weight_sums[:, proj_cols:]
    owned_both = jnp.stack(
        [mixed_own.reshape(per_owner, TILE, width), input_own.reshape(per_owner, TILE, width)],
        axis=1,
    )
    home = lax.all_to_all(
        select_tiles(owned_both, back_index, back_valid),
        "users",
        split_axis=0,
        concat_axis=0,
        tiled=True,
    )
    home_flat = home.reshape(-1, TILE, width)
    mixed = jnp.take(home_flat, 2 * home_index, axis=0, mode="clip").reshape(rows, width)
    input_grad = jnp.take(home_flat, 2 * home_index + 1, axis=0, mode="clip").reshape(rows, width)
    return (mixed, input_grad, proj_sum * norm_factor, out_sum * norm_factor)


def solution(mesh):
    placed = (
        P("users", "heads"),
        P("users", "heads"),
        P(),
        P(None, "heads", None),
        P("heads", None),
        P(),
        P("users"),
        P("users"),
    )
    return jax.shard_map(
        per_device,
        mesh=mesh,
        in_specs=placed,
        out_specs=(
            P("users", "heads"),
            P("users", "heads"),
            P("users", "heads", None),
            P("users", "heads"),
        ),
        check_vma=False,
    )
```
